128 devices in a mesh: tm: 32 (over x, z, core), feat: 4 (over y).
Axes of the slice: x: 4, y: 4, z: 4, core: 2. Of those that a mesh axis runs over, the one named last changes fastest.
Arguments:
- activations: bfloat16 [81920, 2048], P(('tm', 'feat')), may hold values from -19 to 19
- targets: bfloat16 [81920, 128], P(('tm', 'feat')), may hold values from -8 to 8
- span_of: int32 [81920], P(('tm', 'feat')), may hold values from 0 to 31, as said below
Outputs:
- predictions: bfloat16 [81920, 128], P(('tm', 'feat'))
- surprise: float32 [81920], P(('tm', 'feat'))
The draws below stay inside these ranges and needn't reach their ends.
Inputs may be any that keep to these rules, and one draw needn't show every extreme that they name: `span_of`: in each aligned block of 640 rows (the rows of one device) every span from 0 to 31 appears exactly 20 times.
All inputs are finite; a program needn't handle non-finite values.
Results may differ from the reference program's by a relative error of at most 0.0049.
Values may be sent and summed in bfloat16 or wider, within the bound.
No kernel may reach another device: no remote copies, remote signals or barrier semaphores. Data moves between devices by JAX's collectives and lax.ppermute only.
A program may use at most 320 MiB of HBM per device.

```python
import jax
import jax.numpy as jnp
from jax import lax

D = 2048
K = 128
ITERS = 3
TOK_DEV = 640
SPANS = 32
SPAN_SHARE = 20
SPAN_ROWS = 2560
TOKENS = 81920


def latent_field(key):
    base = jax.random.fold_in(key, 11)
    field = jnp.clip(jax.random.normal(base, (TOKENS, D), jnp.float32), -6.0, 6.0)
    return field


def draw_activations(key, part):
    field = latent_field(key)
    spread = jax.random.uniform(jax.random.fold_in(key, 12), (D,), jnp.float32, -1.15, 1.15)
    return (field * jnp.exp(spread)).astype(jnp.bfloat16)


def draw_targets(key, part):
    field = latent_field(key)
    picks = jax.random.randint(jax.random.fold_in(key, 13), (4, K), 0, D)
    coefs = 0.5 * jnp.clip(jax.random.normal(jax.random.fold_in(key, 14), (4, K), jnp.float32), -3.0, 3.0)
    noise = jnp.clip(jax.random.normal(jax.random.fold_in(key, 15), (TOKENS, K), jnp.float32), -6.0, 6.0)
    total = 0.5 * noise
    for slot in range(4):
        total = total + 0.8 * coefs[slot] * jnp.take(field, picks[slot], axis=1)
    return jnp.clip(total, -8.0, 8.0).astype(jnp.bfloat16)


def draw_span_of(key, part):
    blocks = TOKENS // TOK_DEV
    pattern = (jnp.arange(TOK_DEV, dtype=jnp.int32) // SPAN_SHARE).astype(jnp.int32)
    keys = jax.random.split(jax.random.fold_in(key, 21), blocks)
    mixed = jax.vmap(lambda single: jax.random.permutation(single, pattern))(keys)
    return mixed.reshape(-1).astype(jnp.int32)


def setup_inputs(seed: int = 0) -> dict:
    streams_of = jax.random.split(jax.random.key(seed), 4)
    return {
        "activations": draw_activations(jax.random.fold_in(streams_of[3], 71), 0),
        "targets": draw_targets(jax.random.fold_in(streams_of[3], 71), 0),
        "span_of": draw_span_of(jax.random.fold_in(streams_of[3], 71), 0),
    }


RIDGE = 0.1
TINY = 1e-6


def solve_span(gram_prefix, cross_prefix, seen):
    scale = 1.0 / jnp.maximum(seen, 1.0)
    rhs = scale * cross_prefix
    residual = rhs
    direction = rhs
    norm_now = jnp.sum(residual * residual, axis=0)
    solution = jnp.zeros_like(rhs)
    for step in range(ITERS):
        image = scale * jnp.dot(gram_prefix, direction, precision=lax.Precision.HIGHEST, preferred_element_type=jnp.float32) + RIDGE * direction
        alpha = norm_now / (jnp.sum(direction * image, axis=0) + TINY)
        solution = solution + alpha * direction
        if step + 1 < ITERS:
            residual = residual - alpha * image
            norm_next = jnp.sum(residual * residual, axis=0)
            direction = residual + (norm_next / (norm_now + TINY)) * direction
            norm_now = norm_next
    return solution


def reference(activations, targets, span_of):
    order = jnp.argsort(span_of, stable=True).astype(jnp.int32)
    grouped_x = activations[order].reshape(SPANS, SPAN_ROWS, D)
    grouped_y = targets[order].reshape(SPANS, SPAN_ROWS, K)

    def advance(carry, inputs):
        gram_prefix, cross_prefix = carry
        index, rows_x, rows_y = inputs
        seen = (index * SPAN_ROWS).astype(jnp.float32)
        solution = solve_span(gram_prefix, cross_prefix, seen)
        predicted = jnp.dot(rows_x, solution.astype(jnp.bfloat16), preferred_element_type=jnp.float32).astype(jnp.bfloat16)
        wide_x = rows_x.astype(jnp.float32)
        gram_part = jnp.dot(wide_x.T, wide_x, precision=lax.Precision.HIGHEST, preferred_element_type=jnp.float32)
        cross_part = jnp.dot(wide_x.T, rows_y.astype(jnp.float32), precision=lax.Precision.HIGHEST, preferred_element_type=jnp.float32)
        return (gram_prefix + gram_part, cross_prefix + cross_part), predicted

    start = (jnp.zeros((D, D), jnp.float32), jnp.zeros((D, K), jnp.float32))
    indices = jnp.arange(SPANS, dtype=jnp.int32)
    _, predicted = lax.scan(advance, start, (indices, grouped_x, grouped_y))
    predictions = jnp.zeros((TOKENS, K), jnp.bfloat16).at[order].set(predicted.reshape(TOKENS, K))
    error = targets.astype(jnp.float32) - predictions.astype(jnp.float32)
    surprise = jnp.mean(error * error, axis=1)
    return predictions, surprise
```

```python
import jax
import jax.numpy as jnp
from jax import lax
from jax.sharding import Mesh, PartitionSpec as P

ITERS = 3


RIDGE = 0.1
TINY = 1e-06

TM = ("x", "z", "c")
SWAP = [(0, 1), (1, 0)]


def masked_sum(stack, position):
    keep = jnp.arange(stack.shape[0]) < position
    return jnp.sum(jnp.where(keep.reshape((-1,) + (1,) * (stack.ndim - 1)), stack, 0.0), axis=0)


def exclusive_prefix(block):
    ci = lax.axis_index("c")
    zi = lax.axis_index("z")
    xi = lax.axis_index("x")
    rows = block.shape[0]
    half = rows // 2
    partner = lax.ppermute(block, "c", SWAP)
    chip = block + partner
    below = jnp.where(ci == 1, partner, 0.0)
    mine = lax.dynamic_slice_in_dim(chip, ci * half, half, 0)
    along_z = lax.all_gather(mine, "z")
    before_z = masked_sum(along_z, zi)
    total_z = jnp.sum(along_z, axis=0)
    along_x = lax.all_gather(total_z, "x")
    before_x = masked_sum(along_x, xi)
    mine_prefix = before_x + before_z
    other_prefix = lax.ppermute(mine_prefix, "c", SWAP)
    joined = jnp.zeros((rows,) + block.shape[1:], block.dtype)
    joined = lax.dynamic_update_slice_in_dim(joined, mine_prefix, ci * half, 0)
    joined = lax.dynamic_update_slice_in_dim(joined, other_prefix, (1 - ci) * half, 0)
    return joined + below


def body(activations, targets, span_of):
    spans = lax.axis_size(TM)
    feat_count = lax.axis_size("feat")
    tok_dev, width = activations.shape
    n_targets = targets.shape[1]
    block_rows = width // feat_count
    share = tok_dev // spans
    contract = (((0,), (0,)), ((), ()))
    highest = lax.Precision.HIGHEST
    order = jnp.argsort(span_of, stable=True)
    sorted_x = jnp.take(activations, order, axis=0).reshape(spans, share, width)
    sorted_y = jnp.take(targets, order, axis=0).reshape(spans, share, n_targets)
    moved_x, moved_y = (
        lax.all_to_all(sorted_x, TM, split_axis=0, concat_axis=0, tiled=True),
        lax.all_to_all(sorted_y, TM, split_axis=0, concat_axis=0, tiled=True),
    )
    local_x = moved_x.reshape(tok_dev, width)
    local_y = moved_y.reshape(tok_dev, n_targets)
    col_start = lax.axis_index("feat") * block_rows
    rows_x = lax.all_gather(local_x, "feat", axis=0, tiled=True)
    rows_y = lax.all_gather(local_y, "feat", axis=0, tiled=True)
    own = lax.dynamic_slice_in_dim(rows_x, col_start, block_rows, 1)
    gram_part = lax.dot_general(own, rows_x, contract, preferred_element_type=jnp.float32)
    cross_part = lax.dot_general(own, rows_y, contract, preferred_element_type=jnp.float32)

    gram_prefix = exclusive_prefix(gram_part)
    cross_prefix = exclusive_prefix(cross_part)
    span = (lax.axis_index("x") * lax.axis_size("z") + lax.axis_index("z")) * lax.axis_size("c") + lax.axis_index("c")
    seen = (span * (tok_dev * feat_count)).astype(jnp.float32)
    scale = 1.0 / jnp.maximum(seen, 1.0)
    rhs = scale * cross_prefix

    def column_dot(left, right):
        return lax.psum(jnp.sum(left * right, axis=0), "feat")

    residual = rhs
    direction = rhs
    norm_now = column_dot(residual, residual)
    solution = None
    for step in range(ITERS):
        product = jnp.dot(
            gram_prefix,
            lax.all_gather(direction, "feat", axis=0, tiled=True),
            precision=highest,
            preferred_element_type=jnp.float32,
        )
        image = scale * product + RIDGE * direction
        alpha = norm_now / (column_dot(direction, image) + TINY)
        update = alpha * direction
        solution = update if solution is None else solution + update
        if step + 1 < ITERS:
            residual = residual - alpha * image
            norm_next = column_dot(residual, residual)
            direction = residual + norm_next / (norm_now + TINY) * direction
            norm_now = norm_next
    weights = lax.all_gather(solution.astype(jnp.bfloat16), "feat", axis=0, tiled=True)
    predicted = jnp.dot(local_x, weights, preferred_element_type=jnp.float32).astype(jnp.bfloat16)
    returned = lax.all_to_all(
        predicted.reshape(spans, share, n_targets), TM, split_axis=0, concat_axis=0, tiled=True
    )
    in_order = returned.reshape(tok_dev, n_targets)
    predictions = jnp.zeros_like(in_order).at[order].set(in_order)
    error = targets.astype(jnp.float32) - predictions.astype(jnp.float32)
    surprise = jnp.mean(error * error, axis=1)
    return (predictions, surprise)


def solution(mesh):
    tm = mesh.shape["tm"]
    feat = mesh.shape["feat"]
    fine = Mesh(mesh.devices.reshape(tm // 8, 4, 2, feat), TM + ("feat",))
    rows = TM + ("feat",)
    return jax.shard_map(
        body,
        mesh=fine,
        in_specs=(P(rows, None), P(rows, None), P(rows)),
        out_specs=(P(rows, None), P(rows)),
        check_vma=False,
    )
```

```python
import jax
import jax.numpy as jnp
from jax import lax
from jax.sharding import Mesh, PartitionSpec as P

ITERS = 3


RIDGE = 0.1
TINY = 1e-06

TM = ("x", "z", "c")
SWAP = [(0, 1), (1, 0)]


def masked_sum(stack, position):
    keep = jnp.arange(stack.shape[0]) < position
    return jnp.sum(jnp.where(keep.reshape((-1,) + (1,) * (stack.ndim - 1)), stack, 0.0), axis=0)


def exclusive_prefix(block):
    ci = lax.axis_index("c")
    zi = lax.axis_index("z")
    xi = lax.axis_index("x")
    rows = block.shape[0]
    half = rows // 2
    partner = lax.ppermute(block, "c", SWAP)
    chip = block + partner
    below = jnp.where(ci == 1, partner, 0.0)
    mine = lax.dynamic_slice_in_dim(chip, ci * half, half, 0)
    along_z = lax.all_gather(mine, "z")
    before_z = masked_sum(along_z, zi)
    total_z = jnp.sum(along_z, axis=0)
    along_x = lax.all_gather(total_z, "x")
    before_x = masked_sum(along_x, xi)
    mine_prefix = before_x + before_z
    other_prefix = lax.ppermute(mine_prefix, "c", SWAP)
    joined = jnp.zeros((rows,) + block.shape[1:], block.dtype)
    joined = lax.dynamic_update_slice_in_dim(joined, mine_prefix, ci * half, 0)
    joined = lax.dynamic_update_slice_in_dim(joined, other_prefix, (1 - ci) * half, 0)
    return joined + below


def body(activations, targets, span_of):
    spans = lax.axis_size(TM)
    feat_count = lax.axis_size("feat")
    tok_dev, width = activations.shape
    n_targets = targets.shape[1]
    block_rows = width // feat_count
    share = tok_dev // spans
    contract = (((0,), (0,)), ((), ()))
    highest = lax.Precision.HIGHEST
    order = jnp.argsort(span_of, stable=True)
    sorted_x = jnp.take(activations, order, axis=0).reshape(spans, share, width)
    sorted_y = jnp.take(targets, order, axis=0).reshape(spans, share, n_targets)
    moved_x, moved_y = (
        lax.all_to_all(sorted_x, TM, split_axis=0, concat_axis=0, tiled=True),
        lax.all_to_all(sorted_y, TM, split_axis=0, concat_axis=0, tiled=True),
    )
    local_x = moved_x.reshape(tok_dev, width)
    local_y = moved_y.reshape(tok_dev, n_targets)
    col_start = lax.axis_index("feat") * block_rows
    rows_x = lax.all_gather(local_x, "feat", axis=0, tiled=True)
    rows_y = lax.all_gather(local_y, "feat", axis=0, tiled=True)
    own = lax.dynamic_slice_in_dim(rows_x, col_start, block_rows, 1)
    gram_part = lax.dot_general(own, rows_x, contract, preferred_element_type=jnp.float32)
    cross_part = lax.dot_general(own, rows_y, contract, preferred_element_type=jnp.float32)
    moments = exclusive_prefix(jnp.concatenate([gram_part, cross_part], axis=1))
    gram_prefix = moments[:, :width]
    cross_prefix = lax.all_gather(moments[:, width:], "feat", axis=0, tiled=True)
    span = (lax.axis_index("x") * lax.axis_size("z") + lax.axis_index("z")) * lax.axis_size("c") + lax.axis_index("c")
    seen = (span * (tok_dev * feat_count)).astype(jnp.float32)
    scale = 1.0 / jnp.maximum(seen, 1.0)
    rhs = scale * cross_prefix

    residual = rhs
    direction = rhs
    norm_now = jnp.sum(residual * residual, axis=0)
    solution = None
    for step in range(ITERS):
        product = jnp.dot(gram_prefix, direction, precision=highest, preferred_element_type=jnp.float32)
        own_dir = lax.dynamic_slice_in_dim(direction, col_start, block_rows, 0)
        image = lax.all_gather(scale * product + RIDGE * own_dir, "feat", axis=0, tiled=True)
        alpha = norm_now / (jnp.sum(direction * image, axis=0) + TINY)
        update = alpha * direction
        solution = update if solution is None else solution + update
        if step + 1 < ITERS:
            residual = residual - alpha * image
            norm_next = jnp.sum(residual * residual, axis=0)
            direction = residual + norm_next / (norm_now + TINY) * direction
            norm_now = norm_next
    weights = solution.astype(jnp.bfloat16)
    predicted = jnp.dot(local_x, weights, preferred_element_type=jnp.float32).astype(jnp.bfloat16)
    returned = lax.all_to_all(
        predicted.reshape(spans, share, n_targets), TM, split_axis=0, concat_axis=0, tiled=True
    )
    in_order = returned.reshape(tok_dev, n_targets)
    predictions = jnp.zeros_like(in_order).at[order].set(in_order)
    error = targets.astype(jnp.float32) - predictions.astype(jnp.float32)
    surprise = jnp.mean(error * error, axis=1)
    return (predictions, surprise)


def solution(mesh):
    tm = mesh.shape["tm"]
    feat = mesh.shape["feat"]
    fine = Mesh(mesh.devices.reshape(tm // 8, 4, 2, feat), TM + ("feat",))
    rows = TM + ("feat",)
    return jax.shard_map(
        body,
        mesh=fine,
        in_specs=(P(rows, None), P(rows, None), P(rows)),
        out_specs=(P(rows, None), P(rows)),
        check_vma=False,
    )
```

```python
import jax
import jax.numpy as jnp
from jax import lax
from jax.sharding import Mesh, PartitionSpec as P

ITERS = 3


RIDGE = 0.1
TINY = 1e-06

TM = ("x", "z", "c")
SWAP = [(0, 1), (1, 0)]


def masked_sum(stack, position):
    keep = jnp.arange(stack.shape[0]) < position
    return jnp.sum(jnp.where(keep.reshape((-1,) + (1,) * (stack.ndim - 1)), stack, 0.0), axis=0)


def exclusive_prefix(block):
    ci = lax.axis_index("c")
    zi = lax.axis_index("z")
    xi = lax.axis_index("x")
    rows = block.shape[0]
    half = rows // 2
    partner = lax.ppermute(block, "c", SWAP)
    chip = block + partner
    below = jnp.where(ci == 1, partner, 0.0)
    mine = lax.dynamic_slice_in_dim(chip, ci * half, half, 0)
    along_z = lax.all_gather(mine, "z")
    before_z = masked_sum(along_z, zi)
    total_z = jnp.sum(along_z, axis=0)
    quarter = half // lax.axis_size("z")
    piece = lax.dynamic_slice_in_dim(total_z, zi * quarter, quarter, 0)
    along_x = lax.all_gather(piece, "x")
    before_x = lax.all_gather(masked_sum(along_x, xi), "z", axis=0, tiled=True)
    mine_prefix = before_x + before_z
    other_prefix = lax.ppermute(mine_prefix, "c", SWAP)
    joined = jnp.zeros((rows,) + block.shape[1:], block.dtype)
    joined = lax.dynamic_update_slice_in_dim(joined, mine_prefix, ci * half, 0)
    joined = lax.dynamic_update_slice_in_dim(joined, other_prefix, (1 - ci) * half, 0)
    return joined + below


def body(activations, targets, span_of):
    spans = lax.axis_size(TM)
    feat_count = lax.axis_size("feat")
    tok_dev, width = activations.shape
    n_targets = targets.shape[1]
    block_rows = width // feat_count
    share = tok_dev // spans
    contract = (((0,), (0,)), ((), ()))
    highest = lax.Precision.HIGHEST
    order = jnp.argsort(span_of, stable=True)
    sorted_x = jnp.take(activations, order, axis=0).reshape(spans, share, width)
    sorted_y = jnp.take(targets, order, axis=0).reshape(spans, share, n_targets)
    moved_x, moved_y = (
        lax.all_to_all(sorted_x, TM, split_axis=0, concat_axis=0, tiled=True),
        lax.all_to_all(sorted_y, TM, split_axis=0, concat_axis=0, tiled=True),
    )
    local_x = moved_x.reshape(tok_dev, width)
    local_y = moved_y.reshape(tok_dev, n_targets)
    col_start = lax.axis_index("feat") * block_rows
    rows_x = lax.all_gather(local_x, "feat", axis=0, tiled=True)
    rows_y = lax.all_gather(local_y, "feat", axis=0, tiled=True)
    own = lax.dynamic_slice_in_dim(rows_x, col_start, block_rows, 1)
    gram_part = lax.dot_general(own, rows_x, contract, preferred_element_type=jnp.float32)
    cross_part = lax.dot_general(own, rows_y, contract, preferred_element_type=jnp.float32)
    moments = exclusive_prefix(jnp.concatenate([gram_part, cross_part], axis=1))
    gram_prefix = moments[:, :width]
    cross_prefix = lax.all_gather(moments[:, width:], "feat", axis=0, tiled=True)
    span = (lax.axis_index("x") * lax.axis_size("z") + lax.axis_index("z")) * lax.axis_size("c") + lax.axis_index("c")
    seen = (span * (tok_dev * feat_count)).astype(jnp.float32)
    scale = 1.0 / jnp.maximum(seen, 1.0)
    rhs = scale * cross_prefix

    residual = rhs
    direction = rhs
    norm_now = jnp.sum(residual * residual, axis=0)
    solution = None
    for step in range(ITERS):
        product = jnp.dot(gram_prefix, direction, precision=highest, preferred_element_type=jnp.float32)
        own_dir = lax.dynamic_slice_in_dim(direction, col_start, block_rows, 0)
        image = lax.all_gather(scale * product + RIDGE * own_dir, "feat", axis=0, tiled=True)
        alpha = norm_now / (jnp.sum(direction * image, axis=0) + TINY)
        update = alpha * direction
        solution = update if solution is None else solution + update
        if step + 1 < ITERS:
            residual = residual - alpha * image
            norm_next = jnp.sum(residual * residual, axis=0)
            direction = residual + norm_next / (norm_now + TINY) * direction
            norm_now = norm_next
    weights = solution.astype(jnp.bfloat16)
    predicted = jnp.dot(local_x, weights, preferred_element_type=jnp.float32).astype(jnp.bfloat16)
    returned = lax.all_to_all(
        predicted.reshape(spans, share, n_targets), TM, split_axis=0, concat_axis=0, tiled=True
    )
    in_order = returned.reshape(tok_dev, n_targets)
    predictions = jnp.zeros_like(in_order).at[order].set(in_order)
    error = targets.astype(jnp.float32) - predictions.astype(jnp.float32)
    surprise = jnp.mean(error * error, axis=1)
    return (predictions, surprise)


def solution(mesh):
    tm = mesh.shape["tm"]
    feat = mesh.shape["feat"]
    fine = Mesh(mesh.devices.reshape(tm // 8, 4, 2, feat), TM + ("feat",))
    rows = TM + ("feat",)
    return jax.shard_map(
        body,
        mesh=fine,
        in_specs=(P(rows, None), P(rows, None), P(rows)),
        out_specs=(P(rows, None), P(rows)),
        check_vma=False,
    )
```

```python
import jax
import jax.numpy as jnp
from jax import lax
from jax.sharding import Mesh, PartitionSpec as P

ITERS = 3


RIDGE = 0.1
TINY = 1e-06

TM = ("x", "z", "c")
SWAP = [(0, 1), (1, 0)]


def masked_sum(stack, position):
    keep = jnp.arange(stack.shape[0]) < position
    return jnp.sum(jnp.where(keep.reshape((-1,) + (1,) * (stack.ndim - 1)), stack, 0.0), axis=0)


def gather_feat(piece):
    n = lax.axis_size("feat")
    f = lax.axis_index("feat")
    parts = [piece] + [lax.ppermute(piece, "feat", [(i, (i + k) % n) for i in range(n)]) for k in range(1, n)]
    stacked = jnp.stack(parts)
    full = jnp.take(stacked, (f - jnp.arange(n)) % n, axis=0)
    return full.reshape((n * piece.shape[0],) + piece.shape[1:])


def exclusive_prefix(block):
    ci = lax.axis_index("c")
    zi = lax.axis_index("z")
    xi = lax.axis_index("x")
    rows = block.shape[0]
    half = rows // 2
    partner = lax.ppermute(block, "c", SWAP)
    chip = block + partner
    below = jnp.where(ci == 1, partner, 0.0)
    mine = lax.dynamic_slice_in_dim(chip, ci * half, half, 0)
    along_z = lax.all_gather(mine, "z")
    before_z = masked_sum(along_z, zi)
    total_z = jnp.sum(along_z, axis=0)
    quarter = half // lax.axis_size("z")
    piece = lax.dynamic_slice_in_dim(total_z, zi * quarter, quarter, 0)
    along_x = lax.all_gather(piece, "x")
    before_x = lax.all_gather(masked_sum(along_x, xi), "z", axis=0, tiled=True)
    mine_prefix = before_x + before_z
    other_prefix = lax.ppermute(mine_prefix, "c", SWAP)
    joined = jnp.zeros((rows,) + block.shape[1:], block.dtype)
    joined = lax.dynamic_update_slice_in_dim(joined, mine_prefix, ci * half, 0)
    joined = lax.dynamic_update_slice_in_dim(joined, other_prefix, (1 - ci) * half, 0)
    return joined + below


def body(activations, targets, span_of):
    spans = lax.axis_size(TM)
    feat_count = lax.axis_size("feat")
    tok_dev, width = activations.shape
    n_targets = targets.shape[1]
    block_rows = width // feat_count
    share = tok_dev // spans
    contract = (((0,), (0,)), ((), ()))
    highest = lax.Precision.HIGHEST
    order = jnp.argsort(span_of, stable=True)
    joined_in = jnp.concatenate([activations, targets], axis=1)
    sorted_xy = jnp.take(joined_in, order, axis=0).reshape(spans, share, width + n_targets)
    moved = lax.all_to_all(sorted_xy, TM, split_axis=0, concat_axis=0, tiled=True)
    local_xy = moved.reshape(tok_dev, width + n_targets)
    local_x = local_xy[:, :width]
    col_start = lax.axis_index("feat") * block_rows
    rows_xy = lax.all_gather(local_xy, "feat", axis=0, tiled=True)
    own = lax.dynamic_slice_in_dim(rows_xy, col_start, block_rows, 1)
    moments = exclusive_prefix(lax.dot_general(own, rows_xy, contract, preferred_element_type=jnp.float32))
    gram_prefix = moments[:, :width]
    cross_prefix = gather_feat(moments[:, width:])
    span = (lax.axis_index("x") * lax.axis_size("z") + lax.axis_index("z")) * lax.axis_size("c") + lax.axis_index("c")
    seen = (span * (tok_dev * feat_count)).astype(jnp.float32)
    scale = 1.0 / jnp.maximum(seen, 1.0)
    rhs = scale * cross_prefix

    residual = rhs
    direction = rhs
    norm_now = jnp.sum(residual * residual, axis=0)
    solution = None
    for step in range(ITERS):
        product = jnp.dot(gram_prefix, direction, precision=highest, preferred_element_type=jnp.float32)
        own_dir = lax.dynamic_slice_in_dim(direction, col_start, block_rows, 0)
        image = gather_feat(scale * product + RIDGE * own_dir)
        alpha = norm_now / (jnp.sum(direction * image, axis=0) + TINY)
        update = alpha * direction
        solution = update if solution is None else solution + update
        if step + 1 < ITERS:
            residual = residual - alpha * image
            norm_next = jnp.sum(residual * residual, axis=0)
            direction = residual + norm_next / (norm_now + TINY) * direction
            norm_now = norm_next
    weights = solution.astype(jnp.bfloat16)
    predicted = jnp.dot(local_x, weights, preferred_element_type=jnp.float32).astype(jnp.bfloat16)
    returned = lax.all_to_all(
        predicted.reshape(spans, share, n_targets), TM, split_axis=0, concat_axis=0, tiled=True
    )
    in_order = returned.reshape(tok_dev, n_targets)
    predictions = jnp.zeros_like(in_order).at[order].set(in_order)
    error = targets.astype(jnp.float32) - predictions.astype(jnp.float32)
    surprise = jnp.mean(error * error, axis=1)
    return (predictions, surprise)


def solution(mesh):
    tm = mesh.shape["tm"]
    feat = mesh.shape["feat"]
    fine = Mesh(mesh.devices.reshape(tm // 8, 4, 2, feat), TM + ("feat",))
    rows = TM + ("feat",)
    return jax.shard_map(
        body,
        mesh=fine,
        in_specs=(P(rows, None), P(rows, None), P(rows)),
        out_specs=(P(rows, None), P(rows)),
        check_vma=False,
    )
```

```python
import jax
import jax.numpy as jnp
from jax import lax
from jax.sharding import Mesh, PartitionSpec as P

ITERS = 3


RIDGE = 0.1
TINY = 1e-06

TM = ("x", "z", "c")
SWAP = [(0, 1), (1, 0)]


def masked_sum(stack, position):
    keep = jnp.arange(stack.shape[0]) < position
    return jnp.sum(jnp.where(keep.reshape((-1,) + (1,) * (stack.ndim - 1)), stack, 0.0), axis=0)


def gather_feat(piece):
    n = lax.axis_size("feat")
    f = lax.axis_index("feat")
    parts = [piece] + [lax.ppermute(piece, "feat", [(i, (i + k) % n) for i in range(n)]) for k in range(1, n)]
    stacked = jnp.stack(parts)
    full = jnp.take(stacked, (f - jnp.arange(n)) % n, axis=0)
    return full.reshape((n * piece.shape[0],) + piece.shape[1:])


def exclusive_prefix(block):
    ci = lax.axis_index("c")
    zi = lax.axis_index("z")
    xi = lax.axis_index("x")
    rows = block.shape[0]
    half = rows // 2
    partner = lax.ppermute(block, "c", SWAP)
    chip = block + partner
    below = jnp.where(ci == 1, partner, 0.0)
    mine = lax.dynamic_slice_in_dim(chip, ci * half, half, 0)
    along_z = lax.all_gather(mine, "z")
    before_z = masked_sum(along_z, zi)
    total_z = jnp.sum(along_z, axis=0)
    quarter = half // lax.axis_size("z")
    piece = lax.dynamic_slice_in_dim(total_z, zi * quarter, quarter, 0)
    along_x = lax.all_gather(piece, "x")
    before_x = lax.all_gather(masked_sum(along_x, xi), "z", axis=0, tiled=True)
    mine_prefix = before_x + before_z
    other_prefix = lax.ppermute(mine_prefix, "c", SWAP)
    joined = jnp.zeros((rows,) + block.shape[1:], block.dtype)
    joined = lax.dynamic_update_slice_in_dim(joined, mine_prefix, ci * half, 0)
    joined = lax.dynamic_update_slice_in_dim(joined, other_prefix, (1 - ci) * half, 0)
    return joined + below


def body(activations, targets, span_of):
    spans = lax.axis_size(TM)
    feat_count = lax.axis_size("feat")
    tok_dev, width = activations.shape
    n_targets = targets.shape[1]
    block_rows = width // feat_count
    share = tok_dev // spans
    contract = (((0,), (0,)), ((), ()))
    highest = lax.Precision.HIGHEST
    order = jnp.argsort(span_of, stable=True)
    joined_in = jnp.concatenate([activations, targets], axis=1)
    sorted_xy = jnp.take(joined_in, order, axis=0).reshape(spans, share, width + n_targets)
    col_start = lax.axis_index("feat") * block_rows
    cut = share // 2
    locals_x = []
    moments = None
    for piece in (sorted_xy[:, :cut], sorted_xy[:, cut:]):
        moved = lax.all_to_all(piece, TM, split_axis=0, concat_axis=0, tiled=True)
        local_xy = moved.reshape(-1, width + n_targets)
        locals_x.append(local_xy[:, :width])
        rows_xy = lax.all_gather(local_xy, "feat", axis=0, tiled=True)
        own = lax.dynamic_slice_in_dim(rows_xy, col_start, block_rows, 1)
        part = lax.dot_general(own, rows_xy, contract, preferred_element_type=jnp.float32)
        moments = part if moments is None else moments + part
    moments = exclusive_prefix(moments)
    gram_prefix = moments[:, :width]
    cross_prefix = gather_feat(moments[:, width:])
    span = (lax.axis_index("x") * lax.axis_size("z") + lax.axis_index("z")) * lax.axis_size("c") + lax.axis_index("c")
    seen = (span * (tok_dev * feat_count)).astype(jnp.float32)
    scale = 1.0 / jnp.maximum(seen, 1.0)
    rhs = scale * cross_prefix

    residual = rhs
    direction = rhs
    norm_now = jnp.sum(residual * residual, axis=0)
    solution = None
    for step in range(ITERS):
        product = jnp.dot(gram_prefix, direction, precision=highest, preferred_element_type=jnp.float32)
        own_dir = lax.dynamic_slice_in_dim(direction, col_start, block_rows, 0)
        image = gather_feat(scale * product + RIDGE * own_dir)
        alpha = norm_now / (jnp.sum(direction * image, axis=0) + TINY)
        update = alpha * direction
        solution = update if solution is None else solution + update
        if step + 1 < ITERS:
            residual = residual - alpha * image
            norm_next = jnp.sum(residual * residual, axis=0)
            direction = residual + norm_next / (norm_now + TINY) * direction
            norm_now = norm_next
    weights = solution.astype(jnp.bfloat16)
    predicted = [
        jnp.dot(lx, weights, preferred_element_type=jnp.float32).astype(jnp.bfloat16).reshape(spans, -1, n_targets)
        for lx in locals_x
    ]
    returned = lax.all_to_all(
        jnp.concatenate(predicted, axis=1), TM, split_axis=0, concat_axis=0, tiled=True
    )
    in_order = returned.reshape(tok_dev, n_targets)
    predictions = jnp.zeros_like(in_order).at[order].set(in_order)
    error = targets.astype(jnp.float32) - predictions.astype(jnp.float32)
    surprise = jnp.mean(error * error, axis=1)
    return (predictions, surprise)


def solution(mesh):
    tm = mesh.shape["tm"]
    feat = mesh.shape["feat"]
    fine = Mesh(mesh.devices.reshape(tm // 8, 4, 2, feat), TM + ("feat",))
    rows = TM + ("feat",)
    return jax.shard_map(
        body,
        mesh=fine,
        in_specs=(P(rows, None), P(rows, None), P(rows)),
        out_specs=(P(rows, None), P(rows)),
        check_vma=False,
    )
```

```python
import jax
import jax.numpy as jnp
from jax import lax
from jax.sharding import Mesh, PartitionSpec as P

ITERS = 3


RIDGE = 0.1
TINY = 1e-06

TM = ("x", "z", "c")
SWAP = [(0, 1), (1, 0)]


def masked_sum(stack, position):
    keep = jnp.arange(stack.shape[0]) < position
    return jnp.sum(jnp.where(keep.reshape((-1,) + (1,) * (stack.ndim - 1)), stack, 0.0), axis=0)


def gather_feat(piece):
    n = lax.axis_size("feat")
    f = lax.axis_index("feat")
    parts = [piece] + [lax.ppermute(piece, "feat", [(i, (i + k) % n) for i in range(n)]) for k in range(1, n)]
    stacked = jnp.stack(parts)
    full = jnp.take(stacked, (f - jnp.arange(n)) % n, axis=0)
    return full.reshape((n * piece.shape[0],) + piece.shape[1:])


def exclusive_prefix(block):
    ci = lax.axis_index("c")
    zi = lax.axis_index("z")
    xi = lax.axis_index("x")
    rows = block.shape[0]
    half = rows // 2
    partner = lax.ppermute(block, "c", SWAP)
    chip = block + partner
    below = jnp.where(ci == 1, partner, 0.0)
    mine = lax.dynamic_slice_in_dim(chip, ci * half, half, 0)
    along_z = lax.all_gather(mine, "z")
    before_z = masked_sum(along_z, zi)
    total_z = jnp.sum(along_z, axis=0)
    quarter = half // lax.axis_size("z")
    piece = lax.dynamic_slice_in_dim(total_z, zi * quarter, quarter, 0)
    along_x = lax.all_gather(piece, "x")
    before_x = lax.all_gather(masked_sum(along_x, xi), "z", axis=0, tiled=True)
    mine_prefix = before_x + before_z
    other_prefix = lax.ppermute(mine_prefix, "c", SWAP)
    first = ci == 0
    top = jnp.where(first, mine_prefix, other_prefix)
    bottom = jnp.where(first, other_prefix, mine_prefix)
    return jnp.concatenate([top, bottom], axis=0) + below


def body(activations, targets, span_of):
    spans = lax.axis_size(TM)
    feat_count = lax.axis_size("feat")
    tok_dev, width = activations.shape
    n_targets = targets.shape[1]
    block_rows = width // feat_count
    share = tok_dev // spans
    contract = (((0,), (0,)), ((), ()))
    highest = lax.Precision.HIGHEST
    order = jnp.argsort(span_of, stable=True)
    joined_in = jnp.concatenate([activations, targets], axis=1)
    sorted_xy = jnp.take(joined_in, order, axis=0).reshape(spans, share, width + n_targets)
    fanned = jnp.broadcast_to(sorted_xy[:, None], (spans, feat_count, share, width + n_targets))
    moved = lax.all_to_all(
        fanned.reshape(spans * feat_count, share, width + n_targets),
        TM + ("feat",), split_axis=0, concat_axis=0, tiled=True,
    )
    rows_xy = moved.reshape(spans * feat_count * share, width + n_targets)
    fi = lax.axis_index("feat")
    by_source = moved.reshape(spans, feat_count, share, width + n_targets)
    local_x = lax.dynamic_index_in_dim(by_source, fi, axis=1, keepdims=False)[:, :, :width].reshape(tok_dev, width)
    col_start = fi * block_rows
    own = lax.dynamic_slice_in_dim(rows_xy, col_start, block_rows, 1)
    moments = exclusive_prefix(lax.dot_general(own, rows_xy, contract, preferred_element_type=jnp.float32))
    gram_prefix = moments[:, :width]
    cross_prefix = gather_feat(moments[:, width:])
    span = (lax.axis_index("x") * lax.axis_size("z") + lax.axis_index("z")) * lax.axis_size("c") + lax.axis_index("c")
    seen = (span * (tok_dev * feat_count)).astype(jnp.float32)
    scale = 1.0 / jnp.maximum(seen, 1.0)
    rhs = scale * cross_prefix

    residual = rhs
    direction = rhs
    norm_now = jnp.sum(residual * residual, axis=0)
    solution = None
    for step in range(ITERS):
        product = jnp.dot(gram_prefix, direction, precision=highest, preferred_element_type=jnp.float32)
        own_dir = lax.dynamic_slice_in_dim(direction, col_start, block_rows, 0)
        image = gather_feat(scale * product + RIDGE * own_dir)
        alpha = norm_now / (jnp.sum(direction * image, axis=0) + TINY)
        update = alpha * direction
        solution = update if solution is None else solution + update
        if step + 1 < ITERS:
            residual = residual - alpha * image
            norm_next = jnp.sum(residual * residual, axis=0)
            direction = residual + norm_next / (norm_now + TINY) * direction
            norm_now = norm_next
    weights = solution.astype(jnp.bfloat16)
    predicted = jnp.dot(local_x, weights, preferred_element_type=jnp.float32).astype(jnp.bfloat16)
    returned = lax.all_to_all(
        predicted.reshape(spans, share, n_targets), TM, split_axis=0, concat_axis=0, tiled=True
    )
    in_order = returned.reshape(tok_dev, n_targets)
    predictions = jnp.zeros_like(in_order).at[order].set(in_order)
    error = targets.astype(jnp.float32) - predictions.astype(jnp.float32)
    surprise = jnp.mean(error * error, axis=1)
    return (predictions, surprise)


def solution(mesh):
    tm = mesh.shape["tm"]
    feat = mesh.shape["feat"]
    fine = Mesh(mesh.devices.reshape(tm // 8, 4, 2, feat), TM + ("feat",))
    rows = TM + ("feat",)
    return jax.shard_map(
        body,
        mesh=fine,
        in_specs=(P(rows, None), P(rows, None), P(rows)),
        out_specs=(P(rows, None), P(rows)),
        check_vma=False,
    )
```

```python
import jax
import jax.numpy as jnp
from jax import lax
from jax.sharding import Mesh, PartitionSpec as P

ITERS = 3


RIDGE = 0.1
TINY = 1e-06

TM = ("x", "z", "c")
SWAP = [(0, 1), (1, 0)]


def masked_sum(stack, position):
    keep = jnp.arange(stack.shape[0]) < position
    return jnp.sum(jnp.where(keep.reshape((-1,) + (1,) * (stack.ndim - 1)), stack, 0.0), axis=0)


def gather_feat(piece):
    n = lax.axis_size("feat")
    f = lax.axis_index("feat")
    parts = [piece] + [lax.ppermute(piece, "feat", [(i, (i + k) % n) for i in range(n)]) for k in range(1, n)]
    stacked = jnp.stack(parts)
    full = jnp.take(stacked, (f - jnp.arange(n)) % n, axis=0)
    return full.reshape((n * piece.shape[0],) + piece.shape[1:])


def exclusive_prefix(block):
    ci = lax.axis_index("c")
    zi = lax.axis_index("z")
    xi = lax.axis_index("x")
    rows = block.shape[0]
    half = rows // 2
    partner = lax.ppermute(block, "c", SWAP)
    chip = block + partner
    below = jnp.where(ci == 1, partner, 0.0)
    mine = lax.dynamic_slice_in_dim(chip, ci * half, half, 0)
    along_z = lax.all_gather(mine, "z")
    before_z = masked_sum(along_z, zi)
    total_z = jnp.sum(along_z, axis=0)
    quarter = half // lax.axis_size("z")
    piece = lax.dynamic_slice_in_dim(total_z, zi * quarter, quarter, 0)
    along_x = lax.all_gather(piece, "x")
    before_x = lax.all_gather(masked_sum(along_x, xi), "z", axis=0, tiled=True)
    mine_prefix = before_x + before_z
    other_prefix = lax.ppermute(mine_prefix, "c", SWAP)
    first = ci == 0
    top = jnp.where(first, mine_prefix, other_prefix)
    bottom = jnp.where(first, other_prefix, mine_prefix)
    return jnp.concatenate([top, bottom], axis=0) + below


def body(activations, targets, span_of):
    spans = lax.axis_size(TM)
    feat_count = lax.axis_size("feat")
    tok_dev, width = activations.shape
    n_targets = targets.shape[1]
    block_rows = width // feat_count
    share = tok_dev // spans
    contract = (((0,), (0,)), ((), ()))
    highest = lax.Precision.HIGHEST
    order = jnp.argsort(span_of, stable=True)
    joined_in = jnp.concatenate([activations, targets], axis=1)
    sorted_xy = jnp.take(joined_in, order, axis=0).reshape(spans, share, width + n_targets)
    moved = lax.all_to_all(sorted_xy, TM, split_axis=0, concat_axis=0, tiled=True)
    local_xy = moved.reshape(tok_dev, width + n_targets)
    local_x = local_xy[:, :width]
    col_start = lax.axis_index("feat") * block_rows
    rows_xy = lax.all_gather(local_xy, "feat", axis=0, tiled=True)
    own = lax.dynamic_slice_in_dim(rows_xy, col_start, block_rows, 1)
    moments = exclusive_prefix(lax.dot_general(own, rows_xy, contract, preferred_element_type=jnp.float32))
    gram_prefix = moments[:, :width]
    cross_prefix = gather_feat(moments[:, width:])
    span = (lax.axis_index("x") * lax.axis_size("z") + lax.axis_index("z")) * lax.axis_size("c") + lax.axis_index("c")
    seen = (span * (tok_dev * feat_count)).astype(jnp.float32)
    scale = 1.0 / jnp.maximum(seen, 1.0)
    rhs = scale * cross_prefix

    chains = 2
    step_cols = n_targets // chains
    residual = [rhs[:, k * step_cols:(k + 1) * step_cols] for k in range(chains)]
    direction = list(residual)
    norm_now = [jnp.sum(r * r, axis=0) for r in residual]
    solution = [None] * chains
    for step in range(ITERS):
        for k in range(chains):
            product = jnp.dot(gram_prefix, direction[k], precision=lax.Precision.HIGH, preferred_element_type=jnp.float32)
            own_dir = lax.dynamic_slice_in_dim(direction[k], col_start, block_rows, 0)
            image = gather_feat(scale * product + RIDGE * own_dir)
            alpha = norm_now[k] / (jnp.sum(direction[k] * image, axis=0) + TINY)
            update = alpha * direction[k]
            solution[k] = update if solution[k] is None else solution[k] + update
            if step + 1 < ITERS:
                residual[k] = residual[k] - alpha * image
                norm_next = jnp.sum(residual[k] * residual[k], axis=0)
                direction[k] = residual[k] + norm_next / (norm_now[k] + TINY) * direction[k]
                norm_now[k] = norm_next
    solution = jnp.concatenate(solution, axis=1)
    weights = solution.astype(jnp.bfloat16)
    predicted = jnp.dot(local_x, weights, preferred_element_type=jnp.float32).astype(jnp.bfloat16)
    returned = lax.all_to_all(
        predicted.reshape(spans, share, n_targets), TM, split_axis=0, concat_axis=0, tiled=True
    )
    in_order = returned.reshape(tok_dev, n_targets)
    predictions = jnp.zeros_like(in_order).at[order].set(in_order)
    error = targets.astype(jnp.float32) - predictions.astype(jnp.float32)
    surprise = jnp.mean(error * error, axis=1)
    return (predictions, surprise)


def solution(mesh):
    tm = mesh.shape["tm"]
    feat = mesh.shape["feat"]
    fine = Mesh(mesh.devices.reshape(tm // 8, 4, 2, feat), TM + ("feat",))
    rows = TM + ("feat",)
    return jax.shard_map(
        body,
        mesh=fine,
        in_specs=(P(rows, None), P(rows, None), P(rows)),
        out_specs=(P(rows, None), P(rows)),
        check_vma=False,
    )
```

```python
import jax
import jax.numpy as jnp
from jax import lax
from jax.sharding import Mesh, PartitionSpec as P

ITERS = 3


RIDGE = 0.1
TINY = 1e-06

TM = ("x", "z", "c")
SWAP = [(0, 1), (1, 0)]


def masked_sum(stack, position):
    keep = jnp.arange(stack.shape[0]) < position
    return jnp.sum(jnp.where(keep.reshape((-1,) + (1,) * (stack.ndim - 1)), stack, 0.0), axis=0)


def gather_feat(piece):
    n = lax.axis_size("feat")
    f = lax.axis_index("feat")
    parts = [piece] + [lax.ppermute(piece, "feat", [(i, (i + k) % n) for i in range(n)]) for k in range(1, n)]
    stacked = jnp.stack(parts)
    full = jnp.take(stacked, (f - jnp.arange(n)) % n, axis=0)
    return full.reshape((n * piece.shape[0],) + piece.shape[1:])


def exclusive_prefix(block):
    ci = lax.axis_index("c")
    zi = lax.axis_index("z")
    xi = lax.axis_index("x")
    rows = block.shape[0]
    half = rows // 2
    partner = lax.ppermute(block, "c", SWAP)
    chip = block + partner
    below = jnp.where(ci == 1, partner, 0.0)
    mine = lax.dynamic_slice_in_dim(chip, ci * half, half, 0)
    along_z = lax.all_gather(mine, "z")
    before_z = masked_sum(along_z, zi)
    total_z = jnp.sum(along_z, axis=0)
    quarter = half // lax.axis_size("z")
    piece = lax.dynamic_slice_in_dim(total_z, zi * quarter, quarter, 0)
    along_x = lax.all_gather(piece, "x")
    before_x = lax.all_gather(masked_sum(along_x, xi), "z", axis=0, tiled=True)
    mine_prefix = before_x + before_z
    other_prefix = lax.ppermute(mine_prefix, "c", SWAP)
    first = ci == 0
    top = jnp.where(first, mine_prefix, other_prefix)
    bottom = jnp.where(first, other_prefix, mine_prefix)
    return jnp.concatenate([top, bottom], axis=0) + below


def pack_unique(moments, width):
    f = lax.axis_index("feat")
    rows = moments.shape[0]
    blocks = 8
    b = width // blocks
    far_row = f // 2
    gram = moments[:, :width].reshape(rows, blocks, b)
    picked = jnp.take(gram, (2 * f + jnp.arange(6)) % blocks, axis=1)
    row0 = picked[:b]
    row1 = picked[b:]
    q0 = row0[:, 0:4].reshape(b, 4 * b)
    q1 = row1[:, 1:5].reshape(b, 4 * b)
    q4 = jnp.where(far_row == 0, row0[:, 4], row1[:, 5])
    cross = moments[:, width:].reshape(b, -1)
    return jnp.concatenate([q0, q1, q4, cross], axis=1)


def unpack_unique(packed, width, n_targets):
    n = lax.axis_size("feat")
    f = lax.axis_index("feat")
    blocks = 8
    b = width // blocks
    far_row = f // 2
    q0 = packed[:, : 4 * b].reshape(b, 4, b)
    q1 = packed[:, 4 * b : 8 * b].reshape(b, 4, b)
    q4 = packed[:, 8 * b : 9 * b]
    cross = packed[:, 9 * b :].reshape(2 * b, n_targets)
    prev = lax.ppermute(
        jnp.stack([q0[:, 2], q1[:, 1], q0[:, 3], q1[:, 2]]), "feat", [(i, (i + 1) % n) for i in range(n)]
    )
    far = lax.ppermute(jnp.stack([q1[:, 3], q4]), "feat", [(i, (i + 2) % n) for i in range(n)])
    far_q4 = far[1].T
    rel0 = jnp.concatenate(
        [q0[:, 0], q0[:, 1], q0[:, 2], q0[:, 3], jnp.where(far_row == 0, q4, far_q4), far[0].T, prev[0].T, prev[1].T],
        axis=1,
    )
    rel1 = jnp.concatenate(
        [q1[:, 0], q1[:, 1], q1[:, 2], q1[:, 3], jnp.where(far_row == 1, q4, far_q4), prev[2].T, prev[3].T, q0[:, 1].T],
        axis=1,
    )
    abs0 = lax.dynamic_slice_in_dim(jnp.concatenate([rel0, rel0], axis=1), ((blocks - 2 * f) % blocks) * b, width, 1)
    abs1 = lax.dynamic_slice_in_dim(jnp.concatenate([rel1, rel1], axis=1), ((blocks - 1 - 2 * f) % blocks) * b, width, 1)
    return jnp.concatenate([abs0, abs1], axis=0), cross


def body(activations, targets, span_of):
    spans = lax.axis_size(TM)
    feat_count = lax.axis_size("feat")
    tok_dev, width = activations.shape
    n_targets = targets.shape[1]
    block_rows = width // feat_count
    share = tok_dev // spans
    contract = (((0,), (0,)), ((), ()))
    highest = lax.Precision.HIGHEST
    order = jnp.argsort(span_of, stable=True)
    joined_in = jnp.concatenate([activations, targets], axis=1)
    sorted_xy = jnp.take(joined_in, order, axis=0).reshape(spans, share, width + n_targets)
    moved = lax.all_to_all(sorted_xy, TM, split_axis=0, concat_axis=0, tiled=True)
    local_xy = moved.reshape(tok_dev, width + n_targets)
    local_x = local_xy[:, :width]
    col_start = lax.axis_index("feat") * block_rows
    rows_xy = lax.all_gather(local_xy, "feat", axis=0, tiled=True)
    own = lax.dynamic_slice_in_dim(rows_xy, col_start, block_rows, 1)
    moments = lax.dot_general(own, rows_xy, contract, preferred_element_type=jnp.float32)
    gram_prefix, cross_block = unpack_unique(exclusive_prefix(pack_unique(moments, width)), width, n_targets)
    cross_prefix = gather_feat(cross_block)
    span = (lax.axis_index("x") * lax.axis_size("z") + lax.axis_index("z")) * lax.axis_size("c") + lax.axis_index("c")
    seen = (span * (tok_dev * feat_count)).astype(jnp.float32)
    scale = 1.0 / jnp.maximum(seen, 1.0)
    rhs = scale * cross_prefix

    residual = rhs
    direction = rhs
    norm_now = jnp.sum(residual * residual, axis=0)
    solution = None
    for step in range(ITERS):
        product = jnp.dot(gram_prefix, direction, precision=highest, preferred_element_type=jnp.float32)
        own_dir = lax.dynamic_slice_in_dim(direction, col_start, block_rows, 0)
        image = gather_feat(scale * product + RIDGE * own_dir)
        alpha = norm_now / (jnp.sum(direction * image, axis=0) + TINY)
        update = alpha * direction
        solution = update if solution is None else solution + update
        if step + 1 < ITERS:
            residual = residual - alpha * image
            norm_next = jnp.sum(residual * residual, axis=0)
            direction = residual + norm_next / (norm_now + TINY) * direction
            norm_now = norm_next
    weights = solution.astype(jnp.bfloat16)
    predicted = jnp.dot(local_x, weights, preferred_element_type=jnp.float32).astype(jnp.bfloat16)
    returned = lax.all_to_all(
        predicted.reshape(spans, share, n_targets), TM, split_axis=0, concat_axis=0, tiled=True
    )
    in_order = returned.reshape(tok_dev, n_targets)
    predictions = jnp.zeros_like(in_order).at[order].set(in_order)
    error = targets.astype(jnp.float32) - predictions.astype(jnp.float32)
    surprise = jnp.mean(error * error, axis=1)
    return (predictions, surprise)


def solution(mesh):
    tm = mesh.shape["tm"]
    feat = mesh.shape["feat"]
    fine = Mesh(mesh.devices.reshape(tm // 8, 4, 2, feat), TM + ("feat",))
    rows = TM + ("feat",)
    return jax.shard_map(
        body,
        mesh=fine,
        in_specs=(P(rows, None), P(rows, None), P(rows)),
        out_specs=(P(rows, None), P(rows)),
        check_vma=False,
    )
```

```python
import jax
import jax.numpy as jnp
from jax import lax
from jax.sharding import Mesh, PartitionSpec as P

ITERS = 3


RIDGE = 0.1
TINY = 1e-06

TM = ("x", "z", "c")
SWAP = [(0, 1), (1, 0)]


def masked_sum(stack, position):
    keep = jnp.arange(stack.shape[0]) < position
    return jnp.sum(jnp.where(keep.reshape((-1,) + (1,) * (stack.ndim - 1)), stack, 0.0), axis=0)


def gather_feat(piece):
    n = lax.axis_size("feat")
    f = lax.axis_index("feat")
    parts = [piece] + [lax.ppermute(piece, "feat", [(i, (i + k) % n) for i in range(n)]) for k in range(1, n)]
    stacked = jnp.stack(parts)
    full = jnp.take(stacked, (f - jnp.arange(n)) % n, axis=0)
    return full.reshape((n * piece.shape[0],) + piece.shape[1:])


def exclusive_prefix(block):
    ci = lax.axis_index("c")
    zi = lax.axis_index("z")
    xi = lax.axis_index("x")
    rows = block.shape[0]
    half = rows // 2
    partner = lax.ppermute(block, "c", SWAP)
    chip = block + partner
    below = jnp.where(ci == 1, partner, 0.0)
    mine = lax.dynamic_slice_in_dim(chip, ci * half, half, 0)
    along_z = lax.all_gather(mine, "z")
    before_z = masked_sum(along_z, zi)
    total_z = jnp.sum(along_z, axis=0)
    quarter = half // lax.axis_size("z")
    piece = lax.dynamic_slice_in_dim(total_z, zi * quarter, quarter, 0)
    along_x = lax.all_gather(piece, "x")
    before_x = lax.all_gather(masked_sum(along_x, xi), "z", axis=0, tiled=True)
    mine_prefix = before_x + before_z
    other_prefix = lax.ppermute(mine_prefix, "c", SWAP)
    first = ci == 0
    top = jnp.where(first, mine_prefix, other_prefix)
    bottom = jnp.where(first, other_prefix, mine_prefix)
    return jnp.concatenate([top, bottom], axis=0) + below


def body(activations, targets, span_of):
    spans = lax.axis_size(TM)
    feat_count = lax.axis_size("feat")
    tok_dev, width = activations.shape
    n_targets = targets.shape[1]
    block_rows = width // feat_count
    share = tok_dev // spans
    contract = (((0,), (0,)), ((), ()))
    highest = lax.Precision.HIGHEST
    hot = (span_of[:, None] == jnp.arange(spans)[None, :]).astype(jnp.float32)
    earlier = (jnp.arange(tok_dev)[:, None] > jnp.arange(tok_dev)[None, :]).astype(jnp.float32)
    before = jnp.dot(earlier, hot, precision=highest, preferred_element_type=jnp.float32)
    rank = jnp.sum(before * hot, axis=1).astype(jnp.int32)
    dest = span_of * share + rank
    permute = (dest[None, :] == jnp.arange(tok_dev)[:, None]).astype(jnp.bfloat16)
    joined_in = jnp.concatenate([activations, targets], axis=1)
    sorted_xy = jnp.dot(permute, joined_in, preferred_element_type=jnp.float32).astype(jnp.bfloat16)
    sorted_xy = sorted_xy.reshape(spans, share, width + n_targets)
    moved = lax.all_to_all(sorted_xy, TM, split_axis=0, concat_axis=0, tiled=True)
    local_xy = moved.reshape(tok_dev, width + n_targets)
    local_x = local_xy[:, :width]
    col_start = lax.axis_index("feat") * block_rows
    rows_xy = lax.all_gather(local_xy, "feat", axis=0, tiled=True)
    own = lax.dynamic_slice_in_dim(rows_xy, col_start, block_rows, 1)
    moments = exclusive_prefix(lax.dot_general(own, rows_xy, contract, preferred_element_type=jnp.float32))
    gram_prefix = moments[:, :width]
    cross_prefix = gather_feat(moments[:, width:])
    span = (lax.axis_index("x") * lax.axis_size("z") + lax.axis_index("z")) * lax.axis_size("c") + lax.axis_index("c")
    seen = (span * (tok_dev * feat_count)).astype(jnp.float32)
    scale = 1.0 / jnp.maximum(seen, 1.0)
    rhs = scale * cross_prefix

    residual = rhs
    direction = rhs
    norm_now = jnp.sum(residual * residual, axis=0)
    solution = None
    for step in range(ITERS):
        product = jnp.dot(gram_prefix, direction, precision=lax.Precision.HIGH, preferred_element_type=jnp.float32)
        own_dir = lax.dynamic_slice_in_dim(direction, col_start, block_rows, 0)
        image = gather_feat(scale * product + RIDGE * own_dir)
        alpha = norm_now / (jnp.sum(direction * image, axis=0) + TINY)
        update = alpha * direction
        solution = update if solution is None else solution + update
        if step + 1 < ITERS:
            residual = residual - alpha * image
            norm_next = jnp.sum(residual * residual, axis=0)
            direction = residual + norm_next / (norm_now + TINY) * direction
            norm_now = norm_next
    weights = solution.astype(jnp.bfloat16)
    predicted = jnp.dot(local_x, weights, preferred_element_type=jnp.float32).astype(jnp.bfloat16)
    returned = lax.all_to_all(
        predicted.reshape(spans, share, n_targets), TM, split_axis=0, concat_axis=0, tiled=True
    )
    in_order = returned.reshape(tok_dev, n_targets)
    predictions = lax.dot_general(
        permute, in_order, (((0,), (0,)), ((), ())), preferred_element_type=jnp.float32
    ).astype(jnp.bfloat16)
    error = targets.astype(jnp.float32) - predictions.astype(jnp.float32)
    surprise = jnp.mean(error * error, axis=1)
    return (predictions, surprise)


def solution(mesh):
    tm = mesh.shape["tm"]
    feat = mesh.shape["feat"]
    fine = Mesh(mesh.devices.reshape(tm // 8, 4, 2, feat), TM + ("feat",))
    rows = TM + ("feat",)
    return jax.shard_map(
        body,
        mesh=fine,
        in_specs=(P(rows, None), P(rows, None), P(rows)),
        out_specs=(P(rows, None), P(rows)),
        check_vma=False,
    )
```

```python
import jax
import jax.numpy as jnp
from jax import lax
from jax.sharding import Mesh, PartitionSpec as P

ITERS = 3


RIDGE = 0.1
TINY = 1e-06

TM = ("x", "z", "c")
SWAP = [(0, 1), (1, 0)]


def masked_sum(stack, position):
    keep = jnp.arange(stack.shape[0]) < position
    return jnp.sum(jnp.where(keep.reshape((-1,) + (1,) * (stack.ndim - 1)), stack, 0.0), axis=0)


def stack_over(piece, axis):
    n = lax.axis_size(axis)
    f = lax.axis_index(axis)
    parts = [piece] + [lax.ppermute(piece, axis, [(i, (i + k) % n) for i in range(n)]) for k in range(1, n)]
    stacked = jnp.stack(parts)
    return jnp.take(stacked, (f - jnp.arange(n)) % n, axis=0)


def gather_feat(piece, axis="feat"):
    full = stack_over(piece, axis)
    return full.reshape((full.shape[0] * piece.shape[0],) + piece.shape[1:])


def exclusive_prefix(block):
    ci = lax.axis_index("c")
    zi = lax.axis_index("z")
    xi = lax.axis_index("x")
    rows = block.shape[0]
    half = rows // 2
    partner = lax.ppermute(block, "c", SWAP)
    chip = block + partner
    below = jnp.where(ci == 1, partner, 0.0)
    mine = lax.dynamic_slice_in_dim(chip, ci * half, half, 0)
    along_z = lax.all_gather(mine, "z")
    before_z = masked_sum(along_z, zi)
    total_z = jnp.sum(along_z, axis=0)
    quarter = half // lax.axis_size("z")
    piece = lax.dynamic_slice_in_dim(total_z, zi * quarter, quarter, 0)
    along_x = stack_over(piece, "x")
    before_x = gather_feat(masked_sum(along_x, xi), "z")
    mine_prefix = before_x + before_z
    other_prefix = lax.ppermute(mine_prefix, "c", SWAP)
    first = ci == 0
    top = jnp.where(first, mine_prefix, other_prefix)
    bottom = jnp.where(first, other_prefix, mine_prefix)
    return jnp.concatenate([top, bottom], axis=0) + below


def body(activations, targets, span_of):
    spans = lax.axis_size(TM)
    feat_count = lax.axis_size("feat")
    tok_dev, width = activations.shape
    n_targets = targets.shape[1]
    block_rows = width // feat_count
    share = tok_dev // spans
    contract = (((0,), (0,)), ((), ()))
    highest = lax.Precision.HIGHEST
    hot = (span_of[:, None] == jnp.arange(spans)[None, :]).astype(jnp.float32)
    earlier = (jnp.arange(tok_dev)[:, None] > jnp.arange(tok_dev)[None, :]).astype(jnp.float32)
    before = jnp.dot(earlier, hot, precision=highest, preferred_element_type=jnp.float32)
    rank = jnp.sum(before * hot, axis=1).astype(jnp.int32)
    dest = span_of * share + rank
    permute = (dest[None, :] == jnp.arange(tok_dev)[:, None]).astype(jnp.bfloat16)
    joined_in = jnp.concatenate([activations, targets], axis=1)
    sorted_xy = jnp.dot(permute, joined_in, preferred_element_type=jnp.float32).astype(jnp.bfloat16)
    sorted_xy = sorted_xy.reshape(spans, share, width + n_targets)
    moved = lax.all_to_all(sorted_xy, TM, split_axis=0, concat_axis=0, tiled=True)
    local_xy = moved.reshape(tok_dev, width + n_targets)
    local_x = local_xy[:, :width]
    col_start = lax.axis_index("feat") * block_rows
    rows_xy = lax.all_gather(local_xy, "feat", axis=0, tiled=True)
    own = lax.dynamic_slice_in_dim(rows_xy, col_start, block_rows, 1)
    moments = exclusive_prefix(lax.dot_general(own, rows_xy, contract, preferred_element_type=jnp.float32))
    gram_prefix = moments[:, :width]
    cross_prefix = gather_feat(moments[:, width:])
    span = (lax.axis_index("x") * lax.axis_size("z") + lax.axis_index("z")) * lax.axis_size("c") + lax.axis_index("c")
    seen = (span * (tok_dev * feat_count)).astype(jnp.float32)
    scale = 1.0 / jnp.maximum(seen, 1.0)
    rhs = scale * cross_prefix

    residual = rhs
    direction = rhs
    norm_now = jnp.sum(residual * residual, axis=0)
    solution = None
    for step in range(ITERS):
        product = jnp.dot(gram_prefix, direction, precision=lax.Precision.HIGH, preferred_element_type=jnp.float32)
        own_dir = lax.dynamic_slice_in_dim(direction, col_start, block_rows, 0)
        image = gather_feat(scale * product + RIDGE * own_dir)
        alpha = norm_now / (jnp.sum(direction * image, axis=0) + TINY)
        update = alpha * direction
        solution = update if solution is None else solution + update
        if step + 1 < ITERS:
            residual = residual - alpha * image
            norm_next = jnp.sum(residual * residual, axis=0)
            direction = residual + norm_next / (norm_now + TINY) * direction
            norm_now = norm_next
    weights = solution.astype(jnp.bfloat16)
    predicted = jnp.dot(local_x, weights, preferred_element_type=jnp.float32).astype(jnp.bfloat16)
    returned = lax.all_to_all(
        predicted.reshape(spans, share, n_targets), TM, split_axis=0, concat_axis=0, tiled=True
    )
    in_order = returned.reshape(tok_dev, n_targets)
    predictions = lax.dot_general(
        permute, in_order, (((0,), (0,)), ((), ())), preferred_element_type=jnp.float32
    ).astype(jnp.bfloat16)
    error = targets.astype(jnp.float32) - predictions.astype(jnp.float32)
    surprise = jnp.mean(error * error, axis=1)
    return (predictions, surprise)


def solution(mesh):
    tm = mesh.shape["tm"]
    feat = mesh.shape["feat"]
    fine = Mesh(mesh.devices.reshape(tm // 8, 4, 2, feat), TM + ("feat",))
    rows = TM + ("feat",)
    return jax.shard_map(
        body,
        mesh=fine,
        in_specs=(P(rows, None), P(rows, None), P(rows)),
        out_specs=(P(rows, None), P(rows)),
        check_vma=False,
    )
```

```python
import jax
import jax.numpy as jnp
from jax import lax
from jax.sharding import Mesh, PartitionSpec as P

ITERS = 3


RIDGE = 0.1
TINY = 1e-06

TM = ("x", "z", "c")
SWAP = [(0, 1), (1, 0)]


def masked_sum(stack, position):
    keep = jnp.arange(stack.shape[0]) < position
    return jnp.sum(jnp.where(keep.reshape((-1,) + (1,) * (stack.ndim - 1)), stack, 0.0), axis=0)


def gather_feat(piece):
    n = lax.axis_size("feat")
    parts = [piece] + [lax.ppermute(piece, "feat", [(i, (i + k) % n) for i in range(n)]) for k in range(1, n)]
    return jnp.concatenate(parts, axis=0)


def own_order(f, n):
    return (f - jnp.arange(n)) % n


def exclusive_prefix(block):
    ci = lax.axis_index("c")
    zi = lax.axis_index("z")
    xi = lax.axis_index("x")
    rows = block.shape[0]
    half = rows // 2
    partner = lax.ppermute(block, "c", SWAP)
    chip = block + partner
    below = jnp.where(ci == 1, partner, 0.0)
    mine = lax.dynamic_slice_in_dim(chip, ci * half, half, 0)
    along_z = lax.all_gather(mine, "z")
    before_z = masked_sum(along_z, zi)
    total_z = jnp.sum(along_z, axis=0)
    quarter = half // lax.axis_size("z")
    piece = lax.dynamic_slice_in_dim(total_z, zi * quarter, quarter, 0)
    along_x = lax.all_gather(piece, "x")
    before_x = lax.all_gather(masked_sum(along_x, xi), "z", axis=0, tiled=True)
    mine_prefix = before_x + before_z
    other_prefix = lax.ppermute(mine_prefix, "c", SWAP)
    first = ci == 0
    top = jnp.where(first, mine_prefix, other_prefix)
    bottom = jnp.where(first, other_prefix, mine_prefix)
    return jnp.concatenate([top, bottom], axis=0) + below


def body(activations, targets, span_of):
    spans = lax.axis_size(TM)
    feat_count = lax.axis_size("feat")
    tok_dev, width = activations.shape
    n_targets = targets.shape[1]
    block_rows = width // feat_count
    share = tok_dev // spans
    contract = (((0,), (0,)), ((), ()))
    highest = lax.Precision.HIGHEST
    hot = (span_of[:, None] == jnp.arange(spans)[None, :]).astype(jnp.float32)
    earlier = (jnp.arange(tok_dev)[:, None] > jnp.arange(tok_dev)[None, :]).astype(jnp.float32)
    before = jnp.dot(earlier, hot, precision=highest, preferred_element_type=jnp.float32)
    rank = jnp.sum(before * hot, axis=1).astype(jnp.int32)
    dest = span_of * share + rank
    permute = (dest[None, :] == jnp.arange(tok_dev)[:, None]).astype(jnp.bfloat16)
    joined_in = jnp.concatenate([activations, targets], axis=1)
    sorted_xy = jnp.dot(permute, joined_in, preferred_element_type=jnp.float32).astype(jnp.bfloat16)
    sorted_xy = sorted_xy.reshape(spans, share, width + n_targets)
    moved = lax.all_to_all(sorted_xy, TM, split_axis=0, concat_axis=0, tiled=True)
    local_xy = moved.reshape(tok_dev, width + n_targets)
    local_x = local_xy[:, :width]
    col_start = lax.axis_index("feat") * block_rows
    rows_xy = lax.all_gather(local_xy, "feat", axis=0, tiled=True)
    own = lax.dynamic_slice_in_dim(rows_xy, col_start, block_rows, 1)
    moments = exclusive_prefix(lax.dot_general(own, rows_xy, contract, preferred_element_type=jnp.float32))
    fi = lax.axis_index("feat")
    gram_prefix = jnp.take(
        moments[:, :width].reshape(block_rows, feat_count, block_rows), own_order(fi, feat_count), axis=1
    ).reshape(block_rows, width)
    cross_prefix = gather_feat(moments[:, width:])
    span = (lax.axis_index("x") * lax.axis_size("z") + lax.axis_index("z")) * lax.axis_size("c") + lax.axis_index("c")
    seen = (span * (tok_dev * feat_count)).astype(jnp.float32)
    scale = 1.0 / jnp.maximum(seen, 1.0)
    rhs = scale * cross_prefix

    residual = rhs
    direction = rhs
    norm_now = jnp.sum(residual * residual, axis=0)
    solution = None
    for step in range(ITERS):
        product = jnp.dot(gram_prefix, direction, precision=lax.Precision.HIGH, preferred_element_type=jnp.float32)
        own_image = scale * product + RIDGE * direction[:block_rows]
        if step + 1 < ITERS:
            image = gather_feat(own_image)
            curvature = jnp.sum(direction * image, axis=0)
        else:
            partial = jnp.sum(direction[:block_rows] * own_image, axis=0, keepdims=True)
            curvature = jnp.sum(gather_feat(partial), axis=0)
        alpha = norm_now / (curvature + TINY)
        update = alpha * direction
        solution = update if solution is None else solution + update
        if step + 1 < ITERS:
            residual = residual - alpha * image
            norm_next = jnp.sum(residual * residual, axis=0)
            direction = residual + norm_next / (norm_now + TINY) * direction
            norm_now = norm_next
    weights = jnp.take(
        solution.astype(jnp.bfloat16).reshape(feat_count, block_rows, n_targets),
        own_order(fi, feat_count), axis=0,
    ).reshape(width, n_targets)
    predicted = jnp.dot(local_x, weights, preferred_element_type=jnp.float32).astype(jnp.bfloat16)
    returned = lax.all_to_all(
        predicted.reshape(spans, share, n_targets), TM, split_axis=0, concat_axis=0, tiled=True
    )
    in_order = returned.reshape(tok_dev, n_targets)
    predictions = lax.dot_general(
        permute, in_order, (((0,), (0,)), ((), ())), preferred_element_type=jnp.float32
    ).astype(jnp.bfloat16)
    error = targets.astype(jnp.float32) - predictions.astype(jnp.float32)
    surprise = jnp.mean(error * error, axis=1)
    return (predictions, surprise)


def solution(mesh):
    tm = mesh.shape["tm"]
    feat = mesh.shape["feat"]
    fine = Mesh(mesh.devices.reshape(tm // 8, 4, 2, feat), TM + ("feat",))
    rows = TM + ("feat",)
    return jax.shard_map(
        body,
        mesh=fine,
        in_specs=(P(rows, None), P(rows, None), P(rows)),
        out_specs=(P(rows, None), P(rows)),
        check_vma=False,
    )
```

```python
import jax
import jax.numpy as jnp
from jax import lax
from jax.sharding import Mesh, PartitionSpec as P

ITERS = 3


RIDGE = 0.1
TINY = 1e-06

TM = ("x", "z", "c")
SWAP = [(0, 1), (1, 0)]


def masked_sum(stack, position):
    keep = jnp.arange(stack.shape[0]) < position
    return jnp.sum(jnp.where(keep.reshape((-1,) + (1,) * (stack.ndim - 1)), stack, 0.0), axis=0)


def gather_feat(piece):
    n = lax.axis_size("feat")
    parts = [piece] + [lax.ppermute(piece, "feat", [(i, (i - k) % n) for i in range(n)]) for k in range(1, n)]
    return jnp.concatenate(parts, axis=0)


def rotate(a, start, size, axis):
    return lax.dynamic_slice_in_dim(jnp.concatenate([a, a], axis=axis), start, size, axis)


def exclusive_prefix(block):
    ci = lax.axis_index("c")
    zi = lax.axis_index("z")
    xi = lax.axis_index("x")
    rows = block.shape[0]
    half = rows // 2
    partner = lax.ppermute(block, "c", SWAP)
    chip = block + partner
    below = jnp.where(ci == 1, partner, 0.0)
    mine = lax.dynamic_slice_in_dim(chip, ci * half, half, 0)
    along_z = lax.all_gather(mine, "z")
    before_z = masked_sum(along_z, zi)
    total_z = jnp.sum(along_z, axis=0)
    quarter = half // lax.axis_size("z")
    piece = lax.dynamic_slice_in_dim(total_z, zi * quarter, quarter, 0)
    along_x = lax.all_gather(piece, "x")
    before_x = lax.all_gather(masked_sum(along_x, xi), "z", axis=0, tiled=True)
    mine_prefix = before_x + before_z
    other_prefix = lax.ppermute(mine_prefix, "c", SWAP)
    first = ci == 0
    top = jnp.where(first, mine_prefix, other_prefix)
    bottom = jnp.where(first, other_prefix, mine_prefix)
    return jnp.concatenate([top, bottom], axis=0) + below


def body(activations, targets, span_of):
    spans = lax.axis_size(TM)
    feat_count = lax.axis_size("feat")
    tok_dev, width = activations.shape
    n_targets = targets.shape[1]
    block_rows = width // feat_count
    share = tok_dev // spans
    contract = (((0,), (0,)), ((), ()))
    highest = lax.Precision.HIGHEST
    hot = (span_of[:, None] == jnp.arange(spans)[None, :]).astype(jnp.float32)
    earlier = (jnp.arange(tok_dev)[:, None] > jnp.arange(tok_dev)[None, :]).astype(jnp.float32)
    before = jnp.dot(earlier, hot, precision=highest, preferred_element_type=jnp.float32)
    rank = jnp.sum(before * hot, axis=1).astype(jnp.int32)
    dest = span_of * share + rank
    permute = (dest[None, :] == jnp.arange(tok_dev)[:, None]).astype(jnp.bfloat16)
    joined_in = jnp.concatenate([activations, targets], axis=1)
    sorted_xy = jnp.dot(permute, joined_in, preferred_element_type=jnp.float32).astype(jnp.bfloat16)
    sorted_xy = sorted_xy.reshape(spans, share, width + n_targets)
    moved = lax.all_to_all(sorted_xy, TM, split_axis=0, concat_axis=0, tiled=True)
    local_xy = moved.reshape(tok_dev, width + n_targets)
    local_x = local_xy[:, :width]
    col_start = lax.axis_index("feat") * block_rows
    rows_xy = lax.all_gather(local_xy, "feat", axis=0, tiled=True)
    own = lax.dynamic_slice_in_dim(rows_xy, col_start, block_rows, 1)
    moments = exclusive_prefix(lax.dot_general(own, rows_xy, contract, preferred_element_type=jnp.float32))
    fi = lax.axis_index("feat")
    gram_prefix = rotate(moments[:, :width], fi * block_rows, width, 1)
    cross_prefix = gather_feat(moments[:, width:])
    span = (lax.axis_index("x") * lax.axis_size("z") + lax.axis_index("z")) * lax.axis_size("c") + lax.axis_index("c")
    seen = (span * (tok_dev * feat_count)).astype(jnp.float32)
    scale = 1.0 / jnp.maximum(seen, 1.0)
    rhs = scale * cross_prefix

    residual = rhs
    direction = rhs
    norm_now = jnp.sum(residual * residual, axis=0)
    solution = None
    for step in range(ITERS):
        product = jnp.dot(gram_prefix, direction, precision=lax.Precision.HIGH, preferred_element_type=jnp.float32)
        own_image = scale * product + RIDGE * direction[:block_rows]
        if step + 1 < ITERS:
            image = gather_feat(own_image)
            curvature = jnp.sum(direction * image, axis=0)
        else:
            partial = jnp.sum(direction[:block_rows] * own_image, axis=0, keepdims=True)
            curvature = jnp.sum(gather_feat(partial), axis=0)
        alpha = norm_now / (curvature + TINY)
        update = alpha * direction
        solution = update if solution is None else solution + update
        if step + 1 < ITERS:
            residual = residual - alpha * image
            norm_next = jnp.sum(residual * residual, axis=0)
            direction = residual + norm_next / (norm_now + TINY) * direction
            norm_now = norm_next
    weights = rotate(solution.astype(jnp.bfloat16), ((feat_count - fi) % feat_count) * block_rows, width, 0)
    predicted = jnp.dot(local_x, weights, preferred_element_type=jnp.float32).astype(jnp.bfloat16)
    returned = lax.all_to_all(
        predicted.reshape(spans, share, n_targets), TM, split_axis=0, concat_axis=0, tiled=True
    )
    in_order = returned.reshape(tok_dev, n_targets)
    predictions = lax.dot_general(
        permute, in_order, (((0,), (0,)), ((), ())), preferred_element_type=jnp.float32
    ).astype(jnp.bfloat16)
    error = targets.astype(jnp.float32) - predictions.astype(jnp.float32)
    surprise = jnp.mean(error * error, axis=1)
    return (predictions, surprise)


def solution(mesh):
    tm = mesh.shape["tm"]
    feat = mesh.shape["feat"]
    fine = Mesh(mesh.devices.reshape(tm // 8, 4, 2, feat), TM + ("feat",))
    rows = TM + ("feat",)
    return jax.shard_map(
        body,
        mesh=fine,
        in_specs=(P(rows, None), P(rows, None), P(rows)),
        out_specs=(P(rows, None), P(rows)),
        check_vma=False,
    )
```

```python
import jax
import jax.numpy as jnp
from jax import lax
from jax.sharding import Mesh, PartitionSpec as P

ITERS = 3


RIDGE = 0.1
TINY = 1e-06

TM = ("x", "z", "c")
SWAP = [(0, 1), (1, 0)]


def masked_sum(stack, position):
    keep = jnp.arange(stack.shape[0]) < position
    return jnp.sum(jnp.where(keep.reshape((-1,) + (1,) * (stack.ndim - 1)), stack, 0.0), axis=0)


def gather_feat(piece):
    n = lax.axis_size("feat")
    parts = [piece] + [lax.ppermute(piece, "feat", [(i, (i - k) % n) for i in range(n)]) for k in range(1, n)]
    return jnp.concatenate(parts, axis=0)


def rotate(a, start, size, axis):
    return lax.dynamic_slice_in_dim(jnp.concatenate([a, a], axis=axis), start, size, axis)


def exclusive_prefix(block):
    ci = lax.axis_index("c")
    zi = lax.axis_index("z")
    xi = lax.axis_index("x")
    rows = block.shape[0]
    half = rows // 2
    wanted = lax.dynamic_slice_in_dim(block, (1 - ci) * half, half, 0)
    partner_half = lax.ppermute(wanted, "c", SWAP)
    mine = lax.dynamic_slice_in_dim(block, ci * half, half, 0) + partner_half
    rest = lax.ppermute(lax.dynamic_slice_in_dim(block, 0, half, 0), "c", [(0, 1)])
    below = jnp.where(ci == 1, jnp.concatenate([rest, partner_half], axis=0), 0.0)
    along_z = lax.all_gather(mine, "z")
    before_z = masked_sum(along_z, zi)
    total_z = jnp.sum(along_z, axis=0)
    quarter = half // lax.axis_size("z")
    piece = lax.dynamic_slice_in_dim(total_z, zi * quarter, quarter, 0)
    along_x = lax.all_gather(piece, ("x", "z")).reshape((lax.axis_size("x"), lax.axis_size("z")) + piece.shape)
    before_x = masked_sum(along_x, xi).reshape(total_z.shape)
    mine_prefix = before_x + before_z
    other_prefix = lax.ppermute(mine_prefix, "c", SWAP)
    first = ci == 0
    top = jnp.where(first, mine_prefix, other_prefix)
    bottom = jnp.where(first, other_prefix, mine_prefix)
    return jnp.concatenate([top, bottom], axis=0) + below


def body(activations, targets, span_of):
    spans = lax.axis_size(TM)
    feat_count = lax.axis_size("feat")
    tok_dev, width = activations.shape
    n_targets = targets.shape[1]
    block_rows = width // feat_count
    share = tok_dev // spans
    contract = (((0,), (0,)), ((), ()))
    highest = lax.Precision.HIGHEST
    hot = (span_of[:, None] == jnp.arange(spans)[None, :]).astype(jnp.float32)
    earlier = (jnp.arange(tok_dev)[:, None] > jnp.arange(tok_dev)[None, :]).astype(jnp.float32)
    before = jnp.dot(earlier, hot, precision=highest, preferred_element_type=jnp.float32)
    rank = jnp.sum(before * hot, axis=1).astype(jnp.int32)
    dest = span_of * share + rank
    permute = (dest[None, :] == jnp.arange(tok_dev)[:, None]).astype(jnp.bfloat16)
    joined_in = jnp.concatenate([activations, targets], axis=1)
    sorted_xy = jnp.dot(permute, joined_in, preferred_element_type=jnp.float32).astype(jnp.bfloat16)
    sorted_xy = sorted_xy.reshape(spans, share, width + n_targets)
    moved = lax.all_to_all(sorted_xy, TM, split_axis=0, concat_axis=0, tiled=True)
    local_xy = moved.reshape(tok_dev, width + n_targets)
    local_x = local_xy[:, :width]
    col_start = lax.axis_index("feat") * block_rows
    rows_xy = lax.all_gather(local_xy, "feat", axis=0, tiled=True)
    own = lax.dynamic_slice_in_dim(rows_xy, col_start, block_rows, 1)
    moments = exclusive_prefix(lax.dot_general(own, rows_xy, contract, preferred_element_type=jnp.float32))
    fi = lax.axis_index("feat")
    gram_prefix = rotate(moments[:, :width], fi * block_rows, width, 1)
    cross_prefix = gather_feat(moments[:, width:])
    span = (lax.axis_index("x") * lax.axis_size("z") + lax.axis_index("z")) * lax.axis_size("c") + lax.axis_index("c")
    seen = (span * (tok_dev * feat_count)).astype(jnp.float32)
    scale = 1.0 / jnp.maximum(seen, 1.0)
    rhs = scale * cross_prefix

    residual = rhs
    direction = rhs
    norm_now = jnp.sum(residual * residual, axis=0)
    solution = None
    for step in range(ITERS):
        product = jnp.dot(gram_prefix, direction, precision=lax.Precision.HIGH, preferred_element_type=jnp.float32)
        own_image = scale * product + RIDGE * direction[:block_rows]
        if step + 1 < ITERS:
            image = gather_feat(own_image)
            curvature = jnp.sum(direction * image, axis=0)
        else:
            partial = jnp.sum(direction[:block_rows] * own_image, axis=0, keepdims=True)
            curvature = jnp.sum(gather_feat(partial), axis=0)
        alpha = norm_now / (curvature + TINY)
        update = alpha * direction
        solution = update if solution is None else solution + update
        if step + 1 < ITERS:
            residual = residual - alpha * image
            norm_next = jnp.sum(residual * residual, axis=0)
            direction = residual + norm_next / (norm_now + TINY) * direction
            norm_now = norm_next
    weights = rotate(solution.astype(jnp.bfloat16), ((feat_count - fi) % feat_count) * block_rows, width, 0)
    predicted = jnp.dot(local_x, weights, preferred_element_type=jnp.float32).astype(jnp.bfloat16)
    returned = lax.all_to_all(
        predicted.reshape(spans, share, n_targets), TM, split_axis=0, concat_axis=0, tiled=True
    )
    in_order = returned.reshape(tok_dev, n_targets)
    predictions = lax.dot_general(
        permute, in_order, (((0,), (0,)), ((), ())), preferred_element_type=jnp.float32
    ).astype(jnp.bfloat16)
    error = targets.astype(jnp.float32) - predictions.astype(jnp.float32)
    surprise = jnp.mean(error * error, axis=1)
    return (predictions, surprise)


def solution(mesh):
    tm = mesh.shape["tm"]
    feat = mesh.shape["feat"]
    fine = Mesh(mesh.devices.reshape(tm // 8, 4, 2, feat), TM + ("feat",))
    rows = TM + ("feat",)
    return jax.shard_map(
        body,
        mesh=fine,
        in_specs=(P(rows, None), P(rows, None), P(rows)),
        out_specs=(P(rows, None), P(rows)),
        check_vma=False,
    )
```

```python
import jax
import jax.numpy as jnp
from jax import lax
from jax.sharding import Mesh, PartitionSpec as P

ITERS = 3


RIDGE = 0.1
TINY = 1e-06

TM = ("x", "z", "c")
SWAP = [(0, 1), (1, 0)]


def masked_sum(stack, position):
    keep = jnp.arange(stack.shape[0]) < position
    return jnp.sum(jnp.where(keep.reshape((-1,) + (1,) * (stack.ndim - 1)), stack, 0.0), axis=0)


def gather_feat(piece):
    n = lax.axis_size("feat")
    parts = [piece] + [lax.ppermute(piece, "feat", [(i, (i - k) % n) for i in range(n)]) for k in range(1, n)]
    return jnp.concatenate(parts, axis=0)


def rotate(a, start, size, axis):
    return lax.dynamic_slice_in_dim(jnp.concatenate([a, a], axis=axis), start, size, axis)


def exclusive_prefix(block):
    ci = lax.axis_index("c")
    zi = lax.axis_index("z")
    xi = lax.axis_index("x")
    rows = block.shape[0]
    half = rows // 2
    partner = lax.ppermute(block, "c", SWAP)
    chip = block + partner
    below = jnp.where(ci == 1, partner, 0.0)
    mine = lax.dynamic_slice_in_dim(chip, ci * half, half, 0)
    along_z = lax.all_gather(mine, "z")
    before_z = masked_sum(along_z, zi)
    total_z = jnp.sum(along_z, axis=0)
    quarter = half // lax.axis_size("z")
    piece = lax.dynamic_slice_in_dim(total_z, zi * quarter, quarter, 0)
    along_x = lax.all_gather(piece, "x")
    before_x = lax.all_gather(masked_sum(along_x, xi), "z", axis=0, tiled=True)
    return before_x + before_z, below


def join_halves(mine_prefix, below):
    other_prefix = lax.ppermute(mine_prefix, "c", SWAP)
    first = lax.axis_index("c") == 0
    top = jnp.where(first, mine_prefix, other_prefix)
    bottom = jnp.where(first, other_prefix, mine_prefix)
    return jnp.concatenate([top, bottom], axis=0) + below


def body(activations, targets, span_of):
    spans = lax.axis_size(TM)
    feat_count = lax.axis_size("feat")
    tok_dev, width = activations.shape
    n_targets = targets.shape[1]
    block_rows = width // feat_count
    share = tok_dev // spans
    contract = (((0,), (0,)), ((), ()))
    highest = lax.Precision.HIGHEST
    hot = (span_of[:, None] == jnp.arange(spans)[None, :]).astype(jnp.float32)
    earlier = (jnp.arange(tok_dev)[:, None] > jnp.arange(tok_dev)[None, :]).astype(jnp.float32)
    before = jnp.dot(earlier, hot, precision=highest, preferred_element_type=jnp.float32)
    rank = jnp.sum(before * hot, axis=1).astype(jnp.int32)
    dest = span_of * share + rank
    permute = (dest[None, :] == jnp.arange(tok_dev)[:, None]).astype(jnp.bfloat16)
    joined_in = jnp.concatenate([activations, targets], axis=1)
    sorted_xy = jnp.dot(permute, joined_in, preferred_element_type=jnp.float32).astype(jnp.bfloat16)
    sorted_xy = sorted_xy.reshape(spans, share, width + n_targets)
    moved = lax.all_to_all(sorted_xy, TM, split_axis=0, concat_axis=0, tiled=True)
    local_xy = moved.reshape(tok_dev, width + n_targets)
    local_x = local_xy[:, :width]
    col_start = lax.axis_index("feat") * block_rows
    rows_xy = lax.all_gather(local_xy, "feat", axis=0, tiled=True)
    own = lax.dynamic_slice_in_dim(rows_xy, col_start, block_rows, 1)
    halves, below = exclusive_prefix(lax.dot_general(own, rows_xy, contract, preferred_element_type=jnp.float32))
    fi = lax.axis_index("feat")
    cross_prefix = gather_feat(join_halves(halves[:, width:], below[:, width:]))
    gram_prefix = rotate(join_halves(halves[:, :width], below[:, :width]), fi * block_rows, width, 1)
    span = (lax.axis_index("x") * lax.axis_size("z") + lax.axis_index("z")) * lax.axis_size("c") + lax.axis_index("c")
    seen = (span * (tok_dev * feat_count)).astype(jnp.float32)
    scale = 1.0 / jnp.maximum(seen, 1.0)
    rhs = scale * cross_prefix

    residual = rhs
    direction = rhs
    norm_now = jnp.sum(residual * residual, axis=0)
    solution = None
    for step in range(ITERS):
        product = jnp.dot(gram_prefix, direction, precision=lax.Precision.HIGH, preferred_element_type=jnp.float32)
        own_image = scale * product + RIDGE * direction[:block_rows]
        if step + 1 < ITERS:
            image = gather_feat(own_image)
            curvature = jnp.sum(direction * image, axis=0)
        else:
            partial = jnp.sum(direction[:block_rows] * own_image, axis=0, keepdims=True)
            curvature = jnp.sum(gather_feat(partial), axis=0)
        alpha = norm_now / (curvature + TINY)
        update = alpha * direction
        solution = update if solution is None else solution + update
        if step + 1 < ITERS:
            residual = residual - alpha * image
            norm_next = jnp.sum(residual * residual, axis=0)
            direction = residual + norm_next / (norm_now + TINY) * direction
            norm_now = norm_next
    weights = rotate(solution.astype(jnp.bfloat16), ((feat_count - fi) % feat_count) * block_rows, width, 0)
    predicted = jnp.dot(local_x, weights, preferred_element_type=jnp.float32).astype(jnp.bfloat16)
    returned = lax.all_to_all(
        predicted.reshape(spans, share, n_targets), TM, split_axis=0, concat_axis=0, tiled=True
    )
    in_order = returned.reshape(tok_dev, n_targets)
    predictions = lax.dot_general(
        permute, in_order, (((0,), (0,)), ((), ())), preferred_element_type=jnp.float32
    ).astype(jnp.bfloat16)
    error = targets.astype(jnp.float32) - predictions.astype(jnp.float32)
    surprise = jnp.mean(error * error, axis=1)
    return (predictions, surprise)


def solution(mesh):
    tm = mesh.shape["tm"]
    feat = mesh.shape["feat"]
    fine = Mesh(mesh.devices.reshape(tm // 8, 4, 2, feat), TM + ("feat",))
    rows = TM + ("feat",)
    return jax.shard_map(
        body,
        mesh=fine,
        in_specs=(P(rows, None), P(rows, None), P(rows)),
        out_specs=(P(rows, None), P(rows)),
        check_vma=False,
    )
```

```python
import jax
import jax.numpy as jnp
from jax import lax
from jax.sharding import Mesh, PartitionSpec as P


ITERS = 3


RIDGE = 0.1
TINY = 1e-06

TM = ("x", "z", "c")
SWAP = [(0, 1), (1, 0)]


def masked_sum(stack, position):
    keep = jnp.arange(stack.shape[0]) < position
    return jnp.sum(jnp.where(keep.reshape((-1,) + (1,) * (stack.ndim - 1)), stack, 0.0), axis=0)


def gather_feat(piece):
    n = lax.axis_size("feat")
    parts = [piece] + [lax.ppermute(piece, "feat", [(i, (i - k) % n) for i in range(n)]) for k in range(1, n)]
    return jnp.concatenate(parts, axis=0)


def rotate(a, start, size, axis):
    return lax.dynamic_slice_in_dim(jnp.concatenate([a, a], axis=axis), start, size, axis)


def stack_over(piece, axis):
    n = lax.axis_size(axis)
    f = lax.axis_index(axis)
    parts = [piece] + [lax.ppermute(piece, axis, [(i, (i + k) % n) for i in range(n)]) for k in range(1, n)]
    return jnp.take(jnp.stack(parts), (f - jnp.arange(n)) % n, axis=0)


def exclusive_prefix(block, stack=lax.all_gather):
    ci = lax.axis_index("c")
    zi = lax.axis_index("z")
    xi = lax.axis_index("x")
    rows = block.shape[0]
    half = rows // 2
    partner = lax.ppermute(block, "c", SWAP)
    chip = block + partner
    below = jnp.where(ci == 1, partner, 0.0)
    mine = lax.dynamic_slice_in_dim(chip, ci * half, half, 0)
    along_z = stack(mine, "z")
    before_z = masked_sum(along_z, zi)
    total_z = jnp.sum(along_z, axis=0)
    quarter = half // lax.axis_size("z")
    piece = lax.dynamic_slice_in_dim(total_z, zi * quarter, quarter, 0)
    along_x = stack(piece, "x")
    summed_x = masked_sum(along_x, xi)
    before_x = stack(summed_x, "z").reshape(total_z.shape)
    mine_prefix = before_x + before_z
    other_prefix = lax.ppermute(mine_prefix, "c", SWAP)
    first = ci == 0
    top = jnp.where(first, mine_prefix, other_prefix)
    bottom = jnp.where(first, other_prefix, mine_prefix)
    return jnp.concatenate([top, bottom], axis=0) + below


def body(activations, targets, span_of):
    spans = lax.axis_size(TM)
    feat_count = lax.axis_size("feat")
    tok_dev, width = activations.shape
    n_targets = targets.shape[1]
    block_rows = width // feat_count
    share = tok_dev // spans
    contract = (((0,), (0,)), ((), ()))
    highest = lax.Precision.HIGHEST
    hot = (span_of[:, None] == jnp.arange(spans)[None, :]).astype(jnp.float32)
    earlier = (jnp.arange(tok_dev)[:, None] > jnp.arange(tok_dev)[None, :]).astype(jnp.float32)
    before = jnp.dot(earlier, hot, precision=highest, preferred_element_type=jnp.float32)
    rank = jnp.sum(before * hot, axis=1).astype(jnp.int32)
    dest = span_of * share + rank
    permute = (dest[None, :] == jnp.arange(tok_dev)[:, None]).astype(jnp.bfloat16)
    joined_in = jnp.concatenate([activations, targets], axis=1)
    sorted_xy = jnp.dot(permute, joined_in, preferred_element_type=jnp.float32).astype(jnp.bfloat16)
    sorted_xy = sorted_xy.reshape(spans, share, width + n_targets)
    moved = lax.all_to_all(sorted_xy, TM, split_axis=0, concat_axis=0, tiled=True)
    local_xy = moved.reshape(tok_dev, width + n_targets)
    local_x = local_xy[:, :width]
    col_start = lax.axis_index("feat") * block_rows
    rows_xy = lax.all_gather(local_xy, "feat", axis=0, tiled=True)
    own = lax.dynamic_slice_in_dim(rows_xy, col_start, block_rows, 1)
    moments = lax.dot_general(own, rows_xy, contract, preferred_element_type=jnp.float32)
    fi = lax.axis_index("feat")
    cross_prefix = gather_feat(exclusive_prefix(moments[:, width:], stack_over))
    gram_prefix = rotate(exclusive_prefix(moments[:, :width]), fi * block_rows, width, 1)
    span = (lax.axis_index("x") * lax.axis_size("z") + lax.axis_index("z")) * lax.axis_size("c") + lax.axis_index("c")
    seen = (span * (tok_dev * feat_count)).astype(jnp.float32)
    scale = 1.0 / jnp.maximum(seen, 1.0)
    rhs = scale * cross_prefix
    first_norm = jnp.sum(rhs * rhs, axis=0)

    residual = rhs
    direction = rhs
    norm_now = first_norm
    solution = None
    for step in range(ITERS):
        product = jnp.dot(gram_prefix, direction, precision=lax.Precision.HIGH, preferred_element_type=jnp.float32)
        own_image = scale * product + RIDGE * direction[:block_rows]
        if step + 1 < ITERS:
            image = gather_feat(own_image)
            curvature = jnp.sum(direction * image, axis=0)
        else:
            partial = jnp.sum(direction[:block_rows] * own_image, axis=0, keepdims=True)
            curvature = jnp.sum(gather_feat(partial), axis=0)
        alpha = norm_now / (curvature + TINY)
        update = alpha * direction
        solution = update if solution is None else solution + update
        if step + 1 < ITERS:
            residual = residual - alpha * image
            norm_next = jnp.sum(residual * residual, axis=0)
            direction = residual + norm_next / (norm_now + TINY) * direction
            norm_now = norm_next
    weights = rotate(solution.astype(jnp.bfloat16), ((feat_count - fi) % feat_count) * block_rows, width, 0)
    predicted = jnp.dot(local_x, weights, preferred_element_type=jnp.float32).astype(jnp.bfloat16)
    returned = lax.all_to_all(
        predicted.reshape(spans, share, n_targets), TM, split_axis=0, concat_axis=0, tiled=True
    )
    in_order = returned.reshape(tok_dev, n_targets)
    predictions = lax.dot_general(
        permute, in_order, (((0,), (0,)), ((), ())), preferred_element_type=jnp.float32
    ).astype(jnp.bfloat16)
    error = targets.astype(jnp.float32) - predictions.astype(jnp.float32)
    surprise = jnp.mean(error * error, axis=1)
    return (predictions, surprise)


def solution(mesh):
    tm = mesh.shape["tm"]
    feat = mesh.shape["feat"]
    fine = Mesh(mesh.devices.reshape(tm // 8, 4, 2, feat), TM + ("feat",))
    rows = TM + ("feat",)
    return jax.shard_map(
        body,
        mesh=fine,
        in_specs=(P(rows, None), P(rows, None), P(rows)),
        out_specs=(P(rows, None), P(rows)),
        check_vma=False,
    )
```

```python
import jax
import jax.numpy as jnp
from jax import lax
from jax.sharding import Mesh, PartitionSpec as P


ITERS = 3


RIDGE = 0.1
TINY = 1e-06

TM = ("x", "z", "c")
SWAP = [(0, 1), (1, 0)]


def masked_sum(stack, position):
    keep = jnp.arange(stack.shape[0]) < position
    return jnp.sum(jnp.where(keep.reshape((-1,) + (1,) * (stack.ndim - 1)), stack, 0.0), axis=0)


def gather_feat(piece):
    n = lax.axis_size("feat")
    parts = [piece] + [lax.ppermute(piece, "feat", [(i, (i - k) % n) for i in range(n)]) for k in range(1, n)]
    return jnp.concatenate(parts, axis=0)


def rotate(a, start, size, axis):
    return lax.dynamic_slice_in_dim(jnp.concatenate([a, a], axis=axis), start, size, axis)


def stack_over(piece, axis):
    n = lax.axis_size(axis)
    f = lax.axis_index(axis)
    parts = [piece] + [lax.ppermute(piece, axis, [(i, (i + k) % n) for i in range(n)]) for k in range(1, n)]
    return jnp.take(jnp.stack(parts), (f - jnp.arange(n)) % n, axis=0)


def exclusive_prefix(block, stack=lax.all_gather):
    ci = lax.axis_index("c")
    zi = lax.axis_index("z")
    xi = lax.axis_index("x")
    rows = block.shape[0]
    half = rows // 2
    partner = lax.ppermute(block, "c", SWAP)
    chip = block + partner
    below = jnp.where(ci == 1, partner, 0.0)
    mine = lax.dynamic_slice_in_dim(chip, ci * half, half, 0)
    along_z = stack(mine, "z")
    before_z = masked_sum(along_z, zi)
    total_z = jnp.sum(along_z, axis=0)
    quarter = half // lax.axis_size("z")
    piece = lax.dynamic_slice_in_dim(total_z, zi * quarter, quarter, 0)
    along_x = stack(piece, "x")
    summed_x = masked_sum(along_x, xi)
    before_x = stack(summed_x, "z").reshape(total_z.shape)
    mine_prefix = before_x + before_z
    other_prefix = lax.ppermute(mine_prefix, "c", SWAP)
    first = ci == 0
    top = jnp.where(first, mine_prefix, other_prefix)
    bottom = jnp.where(first, other_prefix, mine_prefix)
    return jnp.concatenate([top, bottom], axis=0) + below


def body(activations, targets, span_of):
    spans = lax.axis_size(TM)
    feat_count = lax.axis_size("feat")
    tok_dev, width = activations.shape
    n_targets = targets.shape[1]
    block_rows = width // feat_count
    share = tok_dev // spans
    contract = (((0,), (0,)), ((), ()))
    highest = lax.Precision.HIGHEST
    hot = (span_of[:, None] == jnp.arange(spans)[None, :]).astype(jnp.float32)
    earlier = (jnp.arange(tok_dev)[:, None] > jnp.arange(tok_dev)[None, :]).astype(jnp.float32)
    before = jnp.dot(earlier, hot, precision=highest, preferred_element_type=jnp.float32)
    rank = jnp.sum(before * hot, axis=1).astype(jnp.int32)
    dest = span_of * share + rank
    permute = (dest[None, :] == jnp.arange(tok_dev)[:, None]).astype(jnp.bfloat16)
    joined_in = jnp.concatenate([activations, targets], axis=1)
    sorted_xy = jnp.dot(permute, joined_in, preferred_element_type=jnp.float32).astype(jnp.bfloat16)
    sorted_xy = sorted_xy.reshape(spans, share, width + n_targets)
    moved = lax.all_to_all(sorted_xy, TM, split_axis=0, concat_axis=0, tiled=True)
    local_xy = moved.reshape(tok_dev, width + n_targets)
    local_x = local_xy[:, :width]
    col_start = lax.axis_index("feat") * block_rows
    rows_xy = lax.all_gather(local_xy, "feat", axis=0, tiled=True)
    own = lax.dynamic_slice_in_dim(rows_xy, col_start, block_rows, 1)
    gram_part = lax.dot_general(own, rows_xy[:, :width], contract, preferred_element_type=jnp.float32)
    cross_part = lax.dot_general(own, rows_xy[:, width:], contract, preferred_element_type=jnp.float32)
    fi = lax.axis_index("feat")
    cross_prefix = gather_feat(exclusive_prefix(cross_part, stack_over))
    gram_prefix = rotate(exclusive_prefix(gram_part), fi * block_rows, width, 1)
    span = (lax.axis_index("x") * lax.axis_size("z") + lax.axis_index("z")) * lax.axis_size("c") + lax.axis_index("c")
    seen = (span * (tok_dev * feat_count)).astype(jnp.float32)
    scale = 1.0 / jnp.maximum(seen, 1.0)
    rhs = scale * cross_prefix
    first_norm = jnp.sum(rhs * rhs, axis=0)

    residual = rhs
    direction = rhs
    norm_now = first_norm
    solution = None
    for step in range(ITERS):
        product = jnp.dot(gram_prefix, direction, precision=lax.Precision.HIGH, preferred_element_type=jnp.float32)
        own_image = scale * product + RIDGE * direction[:block_rows]
        if step + 1 < ITERS:
            image = gather_feat(own_image)
            curvature = jnp.sum(direction * image, axis=0)
        else:
            partial = jnp.sum(direction[:block_rows] * own_image, axis=0, keepdims=True)
            curvature = jnp.sum(gather_feat(partial), axis=0)
        alpha = norm_now / (curvature + TINY)
        update = alpha * direction
        solution = update if solution is None else solution + update
        if step + 1 < ITERS:
            residual = residual - alpha * image
            norm_next = jnp.sum(residual * residual, axis=0)
            direction = residual + norm_next / (norm_now + TINY) * direction
            norm_now = norm_next
    weights = rotate(solution.astype(jnp.bfloat16), ((feat_count - fi) % feat_count) * block_rows, width, 0)
    predicted = jnp.dot(local_x, weights, preferred_element_type=jnp.float32).astype(jnp.bfloat16)
    returned = lax.all_to_all(
        predicted.reshape(spans, share, n_targets), TM, split_axis=0, concat_axis=0, tiled=True
    )
    in_order = returned.reshape(tok_dev, n_targets)
    predictions = lax.dot_general(
        permute, in_order, (((0,), (0,)), ((), ())), preferred_element_type=jnp.float32
    ).astype(jnp.bfloat16)
    error = targets.astype(jnp.float32) - predictions.astype(jnp.float32)
    surprise = jnp.mean(error * error, axis=1)
    return (predictions, surprise)


def solution(mesh):
    tm = mesh.shape["tm"]
    feat = mesh.shape["feat"]
    fine = Mesh(mesh.devices.reshape(tm // 8, 4, 2, feat), TM + ("feat",))
    rows = TM + ("feat",)
    return jax.shard_map(
        body,
        mesh=fine,
        in_specs=(P(rows, None), P(rows, None), P(rows)),
        out_specs=(P(rows, None), P(rows)),
        check_vma=False,
    )
```

```python
import jax
import jax.numpy as jnp
from jax import lax
from jax.sharding import Mesh, PartitionSpec as P


ITERS = 3


RIDGE = 0.1
TINY = 1e-06

TM = ("x", "z", "c")
SWAP = [(0, 1), (1, 0)]


def masked_sum(stack, position):
    keep = jnp.arange(stack.shape[0]) < position
    return jnp.sum(jnp.where(keep.reshape((-1,) + (1,) * (stack.ndim - 1)), stack, 0.0), axis=0)


def gather_feat(piece):
    n = lax.axis_size("feat")
    parts = [piece] + [lax.ppermute(piece, "feat", [(i, (i - k) % n) for i in range(n)]) for k in range(1, n)]
    return jnp.concatenate(parts, axis=0)


def rotate(a, start, size, axis):
    return lax.dynamic_slice_in_dim(jnp.concatenate([a, a], axis=axis), start, size, axis)


def stack_over(piece, axis):
    n = lax.axis_size(axis)
    f = lax.axis_index(axis)
    parts = [piece] + [lax.ppermute(piece, axis, [(i, (i + k) % n) for i in range(n)]) for k in range(1, n)]
    return jnp.take(jnp.stack(parts), (f - jnp.arange(n)) % n, axis=0)


def core_level(block):
    ci = lax.axis_index("c")
    half = block.shape[0] // 2
    partner = lax.ppermute(block, "c", SWAP)
    chip = block + partner
    below = jnp.where(ci == 1, partner, 0.0)
    return lax.dynamic_slice_in_dim(chip, ci * half, half, 0), below


def core_level_by_halves(left, right):
    ci = lax.axis_index("c")
    half = left.shape[1] // 2
    contract = (((0,), (0,)), ((), ()))
    wanted = lax.dot_general(
        lax.dynamic_slice_in_dim(left, (1 - ci) * half, half, 1), right, contract, preferred_element_type=jnp.float32
    )
    partner_half = lax.ppermute(wanted, "c", SWAP)
    kept = lax.dot_general(
        lax.dynamic_slice_in_dim(left, ci * half, half, 1), right, contract, preferred_element_type=jnp.float32
    )
    mine = kept + partner_half
    rest = lax.ppermute(kept, "c", [(0, 1)])
    below = jnp.where(ci == 1, jnp.concatenate([rest, partner_half], axis=0), 0.0)
    return mine, below


def exclusive_prefix(block, stack=lax.all_gather, first=None):
    ci = lax.axis_index("c")
    zi = lax.axis_index("z")
    xi = lax.axis_index("x")
    mine, below = core_level(block) if first is None else first
    half = mine.shape[0]
    along_z = stack(mine, "z")
    before_z = masked_sum(along_z, zi)
    total_z = jnp.sum(along_z, axis=0)
    quarter = half // lax.axis_size("z")
    piece = lax.dynamic_slice_in_dim(total_z, zi * quarter, quarter, 0)
    along_x = stack(piece, "x")
    summed_x = masked_sum(along_x, xi)
    before_x = stack(summed_x, "z").reshape(total_z.shape)
    mine_prefix = before_x + before_z
    other_prefix = lax.ppermute(mine_prefix, "c", SWAP)
    first = ci == 0
    top = jnp.where(first, mine_prefix, other_prefix)
    bottom = jnp.where(first, other_prefix, mine_prefix)
    return jnp.concatenate([top, bottom], axis=0) + below


def body(activations, targets, span_of):
    spans = lax.axis_size(TM)
    feat_count = lax.axis_size("feat")
    tok_dev, width = activations.shape
    n_targets = targets.shape[1]
    block_rows = width // feat_count
    share = tok_dev // spans
    contract = (((0,), (0,)), ((), ()))
    hot = (span_of[:, None] == jnp.arange(spans)[None, :]).astype(jnp.float32)
    earlier = (jnp.arange(tok_dev)[:, None] > jnp.arange(tok_dev)[None, :]).astype(jnp.float32)
    before = jnp.dot(earlier.astype(jnp.bfloat16), hot.astype(jnp.bfloat16), preferred_element_type=jnp.float32)
    rank = jnp.sum(before * hot, axis=1).astype(jnp.int32)
    dest = span_of * share + rank
    permute = (dest[None, :] == jnp.arange(tok_dev)[:, None]).astype(jnp.bfloat16)
    joined_in = jnp.concatenate([activations, targets], axis=1)
    sorted_xy = jnp.dot(permute, joined_in, preferred_element_type=jnp.float32).astype(jnp.bfloat16)
    sorted_xy = sorted_xy.reshape(spans, share, width + n_targets)
    moved = lax.all_to_all(sorted_xy, TM, split_axis=0, concat_axis=0, tiled=True)
    local_xy = moved.reshape(tok_dev, width + n_targets)
    local_x = local_xy[:, :width]
    col_start = lax.axis_index("feat") * block_rows
    rows_xy = lax.all_gather(local_xy, "feat", axis=0, tiled=True)
    own = lax.dynamic_slice_in_dim(rows_xy, col_start, block_rows, 1)
    cross_part = lax.dot_general(own, rows_xy[:, width:], contract, preferred_element_type=jnp.float32)
    fi = lax.axis_index("feat")
    cross_prefix = gather_feat(exclusive_prefix(cross_part, stack_over))
    first = core_level_by_halves(own, rows_xy[:, :width])
    gram_prefix = rotate(exclusive_prefix(None, first=first), fi * block_rows, width, 1)
    span = (lax.axis_index("x") * lax.axis_size("z") + lax.axis_index("z")) * lax.axis_size("c") + lax.axis_index("c")
    seen = (span * (tok_dev * feat_count)).astype(jnp.float32)
    scale = 1.0 / jnp.maximum(seen, 1.0)
    rhs = scale * cross_prefix
    first_norm = jnp.sum(rhs * rhs, axis=0)

    residual = rhs
    direction = rhs
    norm_now = first_norm
    solution = None
    for step in range(ITERS):
        product = jnp.dot(gram_prefix, direction, precision=lax.Precision.HIGH, preferred_element_type=jnp.float32)
        own_image = scale * product + RIDGE * direction[:block_rows]
        if step + 1 < ITERS:
            image = gather_feat(own_image)
            curvature = jnp.sum(direction * image, axis=0)
        else:
            partial = jnp.sum(direction[:block_rows] * own_image, axis=0, keepdims=True)
            curvature = jnp.sum(gather_feat(partial), axis=0)
        alpha = norm_now / (curvature + TINY)
        update = alpha * direction
        solution = update if solution is None else solution + update
        if step + 1 < ITERS:
            residual = residual - alpha * image
            norm_next = jnp.sum(residual * residual, axis=0)
            direction = residual + norm_next / (norm_now + TINY) * direction
            norm_now = norm_next
    weights = rotate(solution.astype(jnp.bfloat16), ((feat_count - fi) % feat_count) * block_rows, width, 0)
    predicted = jnp.dot(local_x, weights, preferred_element_type=jnp.float32).astype(jnp.bfloat16)
    returned = lax.all_to_all(
        predicted.reshape(spans, share, n_targets), TM, split_axis=0, concat_axis=0, tiled=True
    )
    in_order = returned.reshape(tok_dev, n_targets)
    predictions = lax.dot_general(
        permute, in_order, (((0,), (0,)), ((), ())), preferred_element_type=jnp.float32
    ).astype(jnp.bfloat16)
    error = targets.astype(jnp.float32) - predictions.astype(jnp.float32)
    surprise = jnp.mean(error * error, axis=1)
    return (predictions, surprise)


def solution(mesh):
    tm = mesh.shape["tm"]
    feat = mesh.shape["feat"]
    fine = Mesh(mesh.devices.reshape(tm // 8, 4, 2, feat), TM + ("feat",))
    rows = TM + ("feat",)
    return jax.shard_map(
        body,
        mesh=fine,
        in_specs=(P(rows, None), P(rows, None), P(rows)),
        out_specs=(P(rows, None), P(rows)),
        check_vma=False,
    )
```
